256 devices in a mesh: section: 4 (over z_lo, core), seq: 64 (over y, x, z_hi).
Axes of the slice: x: 4, y: 4, z: 8 (z_hi: 4, z_lo: 2; z = z_hi * 2 + z_lo), core: 2. Of those that a mesh axis runs over, the one named last changes fastest.
Arguments:
- q_img: bfloat16 [8192, 3072], P('seq', 'section'), may hold values from -6 to 6
- k_img: bfloat16 [8192, 3072], P('seq', 'section'), may hold values from -6 to 6
- v_img: bfloat16 [8192, 3072], P('seq', 'section'), may hold values from -6 to 6
- q_txt: bfloat16 [256, 3072], P('seq', 'section'), may hold values from -6 to 6
- k_txt: bfloat16 [256, 3072], P('seq', 'section'), may hold values from -6 to 6
- v_txt: bfloat16 [256, 3072], P('seq', 'section'), may hold values from -6 to 6
- norm_gains: float32 [4, 128], replicated, may hold values from 1.2 to 2
- block_map: int32 [24, 64, 64], P('section', 'seq'), may hold values 0 or 1
Outputs:
- image_out: bfloat16 [2048, 4, 3072], P('seq', 'section')
- text_out: bfloat16 [256, 3072], P('seq', 'section')
The draws below stay inside these ranges and needn't reach their ends.
All inputs are finite; a program needn't handle non-finite values. No bound on the sum of `block_map` on one device may be relied on, other than what follows from the above.
Results may differ from the reference program's by a relative error of at most 0.011.
Values may be sent and summed in bfloat16 or wider, within the bound.
No kernel may reach another device: no remote copies, remote signals or barrier semaphores. Data moves between devices by JAX's collectives and lax.ppermute only.
A program may use at most 256 MiB of HBM per device.

```python
import math
import jax
import jax.numpy as jnp
from jax import lax

HEADS = 24
DH = 128
BLOCK = 128
TXT = 256
IMG = 8192
NB = 64
N_SECTION = 4


def with_ends(entries, stream_key, low, largest):
    extent = entries.shape
    spot = [jax.random.randint(jax.random.fold_in(stream_key, axis), (), 0, extent[axis]) for axis in range(len(extent))]
    entries = entries.at[tuple(spot)].set(low)
    longest = extent.index(max(extent))
    spot[longest] = (spot[longest] + 1) % extent[longest]
    return entries.at[tuple(spot)].set(largest)


def level_of(own_key, extent, cuts, least, largest):
    def one(dim, parts):
        steps = jax.random.uniform(jax.random.fold_in(jax.random.fold_in(own_key, 6), dim), (parts,), jnp.float32, least / len(cuts), largest / len(cuts))
        return jnp.repeat(jnp.exp(steps), extent[dim] // parts).reshape((-1,) + (1,) * (len(extent) - dim - 1))

    level = one(*cuts[0])
    for cut in cuts[1:]:
        level = level * one(*cut)
    return level


def normal_values(own_key, shape, spread, most, cuts=(), kind=jnp.bfloat16):
    drawn = jax.random.normal(own_key, shape, jnp.float32) * spread
    if len(cuts) > 0:
        drawn = level_of(own_key, shape, cuts, -0.22, 0.18) * drawn
    return jnp.clip(drawn, min=-most, max=most).astype(kind)


def setup_inputs(seed: int = 0) -> dict:
    seeds = jax.random.split(jax.random.key(seed), 9)
    q_img = normal_values(seeds[0], (IMG, HEADS * DH), 1.0, 6.0, ((0, 64), (1, 4)))
    k_img = normal_values(seeds[1], (IMG, HEADS * DH), 1.0, 6.0, ((0, 64), (1, 4)))
    v_img = normal_values(seeds[2], (IMG, HEADS * DH), 1.0, 6.0, ((0, 64), (1, 4)))
    q_txt = normal_values(seeds[3], (TXT, HEADS * DH), 1.0, 6.0, ((0, 64), (1, 4)))
    k_txt = normal_values(seeds[4], (TXT, HEADS * DH), 1.0, 6.0, ((0, 64), (1, 4)))
    v_txt = normal_values(seeds[5], (TXT, HEADS * DH), 1.0, 6.0, ((0, 64), (1, 4)))
    norm_gains = jnp.clip(jnp.exp(jax.random.uniform(seeds[6], (4, DH), jnp.float32, math.log(1.2), math.log(2.0))), 1.2, 2.0)
    block_map = with_ends((jax.random.randint(seeds[7], (HEADS, NB, NB), 0, 2) < 1).astype(jnp.int32), jax.random.fold_in(seeds[7], 1), 0, 1)
    return dict(q_img=q_img, k_img=k_img, v_img=v_img, q_txt=q_txt, k_txt=k_txt, v_txt=v_txt, norm_gains=norm_gains, block_map=block_map)


def normed(values, gain):
    rows = values.shape[0]
    floats = values.astype(jnp.float32).reshape(rows, HEADS, DH)
    power = lax.optimization_barrier(jnp.mean(floats * floats, axis=-1, keepdims=True))
    return (floats * lax.rsqrt(power + 1e-06) * gain).astype(jnp.bfloat16)

def reference(q_img, k_img, v_img, q_txt, k_txt, v_txt, norm_gains, block_map):
    queries = jnp.concatenate([normed(q_img, norm_gains[0]), normed(q_txt, norm_gains[2])], axis=0)
    keys_all = jnp.concatenate([normed(k_img, norm_gains[1]), normed(k_txt, norm_gains[3])], axis=0)
    total = IMG + TXT
    values_all = jnp.concatenate([v_img, v_txt], axis=0).reshape(total, HEADS, DH)

    def per_head(pieces):
        query_head, key_head, value_head, flags = pieces
        scores = jnp.dot(query_head, key_head.T, preferred_element_type=jnp.float32) * DH ** (-0.5)
        image_mask = jnp.broadcast_to(flags[:, None, :, None] > 0, (NB, BLOCK, NB, BLOCK)).reshape(IMG, IMG)
        keep = jnp.pad(image_mask, ((0, TXT), (0, TXT)), constant_values=True)
        weights = jnp.where(keep, jnp.exp(scores), jnp.float32(0.0))
        denominator = lax.optimization_barrier(jnp.sum(weights, axis=-1))
        numerator = jnp.dot(weights.astype(jnp.bfloat16), value_head, preferred_element_type=jnp.float32)
        return numerator / denominator[:, None]
    result = lax.map(per_head, (queries.transpose(1, 0, 2), keys_all.transpose(1, 0, 2), values_all.transpose(1, 0, 2), block_map))
    merged = result.transpose(1, 0, 2).reshape(total, HEADS * DH).astype(jnp.bfloat16)
    image_out = merged[:IMG].reshape(IMG // N_SECTION, N_SECTION, HEADS * DH)
    text_out = merged[IMG:]
    return (image_out, text_out)
```

```python
import jax
import jax.numpy as jnp
from jax import lax
from jax.sharding import Mesh, PartitionSpec as P

BLOCK = 128
QUERY_GROUP = 4


def normed(values, gain, heads):
    rows = values.shape[0]
    floats = values.astype(jnp.float32).reshape(rows, heads, gain.shape[0])
    power = jnp.mean(floats * floats, axis=-1, keepdims=True)
    return (floats * lax.rsqrt(power + 1e-06) * gain).astype(jnp.bfloat16)


def body(q_img, k_img, v_img, q_txt, k_txt, v_txt, norm_gains, block_map):
    rows, width = q_img.shape
    head_size = norm_gains.shape[1]
    heads = width // head_size
    text_rows = q_txt.shape[0]
    stride = rows + text_rows
    groups_q = lax.axis_size("qq")
    groups_k = lax.axis_size("kk")
    own_q = lax.axis_index("qq")

    queries = jnp.concatenate(
        [normed(q_img, norm_gains[0], heads), normed(q_txt, norm_gains[2], heads)], axis=0
    )
    keys = jnp.concatenate(
        [normed(k_img, norm_gains[1], heads), normed(k_txt, norm_gains[3], heads)], axis=0
    )
    values = jnp.concatenate([v_img, v_txt], axis=0).reshape(stride, heads, head_size)
    pair = jnp.stack([keys, values], axis=1)

    all_q = lax.all_gather(queries, "qq", axis=0, tiled=True)
    all_kv = lax.all_gather(pair, "kk", axis=0, tiled=True)
    flags = lax.all_gather(block_map, "qq", axis=1, tiled=True)
    flags = flags.reshape(heads, groups_q, groups_k, groups_q)
    flags = lax.dynamic_index_in_dim(flags, own_q, axis=3, keepdims=False)

    all_k = all_kv[:, 0]
    all_v = all_kv[:, 1]
    scores = jnp.einsum(
        "qhd,khd->hqk", all_q, all_k, preferred_element_type=jnp.float32
    ) * head_size ** (-0.5)
    scores = scores.reshape(heads, groups_q, stride, groups_k, stride)
    image_q = jnp.arange(stride) < rows
    text_pair = ~(image_q[:, None, None] & image_q[None, None, :])
    keep = (flags[:, :, None, :, None] > 0) | text_pair[None, None]
    weights = jnp.where(keep, jnp.exp(scores), jnp.float32(0.0))
    denom = jnp.sum(weights, axis=(3, 4)).reshape(heads, groups_q * stride)
    weights = weights.reshape(heads, groups_q * stride, groups_k * stride)
    numer = jnp.einsum(
        "hqk,khd->hqd",
        weights.astype(jnp.bfloat16),
        all_v,
        preferred_element_type=jnp.float32,
    )
    numer = lax.psum_scatter(numer, "qq", scatter_dimension=1, tiled=True)
    denom = lax.psum_scatter(denom, "qq", scatter_dimension=1, tiled=True)
    result = numer / denom[..., None]
    merged = result.transpose(1, 0, 2).reshape(stride, width).astype(jnp.bfloat16)
    image_part = merged[:rows]
    text_out = merged[rows:]
    sections = lax.axis_size("section")
    image_out = lax.all_to_all(
        image_part.reshape(rows // sections, sections, width),
        "section",
        split_axis=1,
        concat_axis=2,
        tiled=True,
    )
    return (image_out, text_out)


def solution(mesh):
    sections, seq = mesh.devices.shape
    grid = Mesh(
        mesh.devices.reshape(sections, seq // QUERY_GROUP, QUERY_GROUP),
        ("section", "kk", "qq"),
    )
    rows = ("kk", "qq")
    placed = (
        P(rows, "section"),
        P(rows, "section"),
        P(rows, "section"),
        P(rows, "section"),
        P(rows, "section"),
        P(rows, "section"),
        P(),
        P("section", rows, None),
    )
    return jax.shard_map(
        body,
        mesh=grid,
        in_specs=placed,
        out_specs=(P(rows, "section", None), P(rows, "section")),
        check_vma=False,
    )
```

```python
import jax
import jax.numpy as jnp
from jax import lax
from jax.experimental import pallas as pl
from jax.experimental.pallas import tpu as pltpu
from jax.sharding import Mesh, PartitionSpec as P

BLOCK = 128
QUERY_GROUP = 4


def normed(values, gain, heads):
    rows = values.shape[0]
    floats = values.astype(jnp.float32).reshape(rows, heads, gain.shape[0])
    power = jnp.mean(floats * floats, axis=-1, keepdims=True)
    return (floats * lax.rsqrt(power + 1e-06) * gain).astype(jnp.bfloat16)


def attend_kernel(qi_ref, qt_ref, ki_ref, kt_ref, vi_ref, vt_ref, fl_ref, ni_ref, nt_ref, di_ref, dt_ref):
    head_size = qi_ref.shape[1]
    scale = head_size ** (-0.5)
    q_blocks = qi_ref.shape[0] // BLOCK
    dims = (((1,), (1,)), ((), ()))
    keys_img = ki_ref[...]
    keys_txt = kt_ref[...]
    vals_img = vi_ref[...]
    vals_txt = vt_ref[...]

    def one(q, flags):
        s_img = lax.dot_general(q, keys_img, dims, preferred_element_type=jnp.float32) * scale
        s_txt = lax.dot_general(q, keys_txt, dims, preferred_element_type=jnp.float32) * scale
        e_img = jnp.exp(s_img)
        if flags is not None:
            e_img = jnp.where(flags > 0, e_img, jnp.float32(0.0))
        e_txt = jnp.exp(s_txt)
        den = jnp.sum(e_img, axis=1, keepdims=True) + jnp.sum(e_txt, axis=1, keepdims=True)
        num = jnp.dot(e_img.astype(jnp.bfloat16), vals_img, preferred_element_type=jnp.float32)
        num = num + jnp.dot(e_txt.astype(jnp.bfloat16), vals_txt, preferred_element_type=jnp.float32)
        return num, den

    for a in range(q_blocks):
        rows = slice(a * BLOCK, (a + 1) * BLOCK)
        num, den = one(qi_ref[rows, :], fl_ref[0, a:a + 1, :])
        ni_ref[rows, :] = num
        di_ref[rows, :] = jnp.broadcast_to(den, num.shape)
    num, den = one(qt_ref[...], None)
    nt_ref[...] = num
    dt_ref[...] = jnp.broadcast_to(den, num.shape)


def attend(qi, qt, ki, kt, vi, vt, fl, heads, head_size):
    def cols(rows):
        return pl.BlockSpec((rows, head_size), lambda h: (0, h))

    n_qi, n_qt, n_ki, n_kt = qi.shape[0], qt.shape[0], ki.shape[0], kt.shape[0]
    width = heads * head_size
    return pl.pallas_call(
        attend_kernel,
        grid=(heads,),
        in_specs=[
            cols(n_qi), cols(n_qt), cols(n_ki), cols(n_kt), cols(n_ki), cols(n_kt),
            pl.BlockSpec((1,) + fl.shape[1:], lambda h: (h, 0, 0)),
        ],
        out_specs=[cols(n_qi), cols(n_qt), cols(n_qi), cols(n_qt)],
        out_shape=[
            jax.ShapeDtypeStruct((n_qi, width), jnp.float32),
            jax.ShapeDtypeStruct((n_qt, width), jnp.float32),
            jax.ShapeDtypeStruct((n_qi, width), jnp.float32),
            jax.ShapeDtypeStruct((n_qt, width), jnp.float32),
        ],
        compiler_params=pltpu.CompilerParams(vmem_limit_bytes=48 * 1024 * 1024),
    )(qi, qt, ki, kt, vi, vt, fl)


def body(q_img, k_img, v_img, q_txt, k_txt, v_txt, norm_gains, block_map):
    rows, width = q_img.shape
    head_size = norm_gains.shape[1]
    heads = width // head_size
    text_rows = q_txt.shape[0]
    stride = rows + text_rows
    groups_q = lax.axis_size("qq")
    groups_k = lax.axis_size("kk")
    own_q = lax.axis_index("qq")

    queries = jnp.concatenate(
        [normed(q_img, norm_gains[0], heads), normed(q_txt, norm_gains[2], heads)], axis=0
    ).reshape(stride, width)
    keys = jnp.concatenate(
        [normed(k_img, norm_gains[1], heads), normed(k_txt, norm_gains[3], heads)], axis=0
    ).reshape(stride, width)
    values = jnp.concatenate([v_img, v_txt], axis=0)
    pair = jnp.stack([keys, values], axis=0)

    all_q = lax.all_gather(queries, "qq", axis=0, tiled=True)
    all_kv = lax.all_gather(pair, "kk", axis=1, tiled=True)
    flags = lax.all_gather(block_map, "qq", axis=1, tiled=True)
    flags = flags.reshape(heads, groups_q, groups_k, groups_q)
    flags = lax.dynamic_index_in_dim(flags, own_q, axis=3, keepdims=False)
    flags = jnp.repeat(flags, BLOCK, axis=2)

    all_q = all_q.reshape(groups_q, stride, width)
    qi = all_q[:, :rows].reshape(groups_q * rows, width)
    qt = all_q[:, rows:].reshape(groups_q * text_rows, width)
    all_kv = all_kv.reshape(2, groups_k, stride, width)
    ki = all_kv[0, :, :rows].reshape(groups_k * rows, width)
    kt = all_kv[0, :, rows:].reshape(groups_k * text_rows, width)
    vi = all_kv[1, :, :rows].reshape(groups_k * rows, width)
    vt = all_kv[1, :, rows:].reshape(groups_k * text_rows, width)

    ni, nt, di, dt = attend(qi, qt, ki, kt, vi, vt, flags, heads, head_size)
    numer = jnp.concatenate(
        [ni.reshape(groups_q, rows, width), nt.reshape(groups_q, text_rows, width)], axis=1
    )
    denom = jnp.concatenate(
        [di[:, ::head_size].reshape(groups_q, rows, heads),
         dt[:, ::head_size].reshape(groups_q, text_rows, heads)], axis=1
    )
    packed = jnp.concatenate([numer, denom], axis=2)
    packed = lax.all_to_all(packed, "qq", split_axis=0, concat_axis=0, tiled=True)
    packed = jnp.sum(packed, axis=0)
    numer = packed[:, :width].reshape(stride, heads, head_size)
    denom = packed[:, width:]
    result = numer / denom[..., None]
    merged = result.reshape(stride, width).astype(jnp.bfloat16)
    image_part = merged[:rows]
    text_out = merged[rows:]
    sections = lax.axis_size("section")
    image_out = lax.all_to_all(
        image_part.reshape(rows // sections, sections, width),
        "section",
        split_axis=1,
        concat_axis=2,
        tiled=True,
    )
    return (image_out, text_out)


def solution(mesh):
    sections, seq = mesh.devices.shape
    grid = Mesh(
        mesh.devices.reshape(sections, seq // QUERY_GROUP, QUERY_GROUP),
        ("section", "kk", "qq"),
    )
    rows = ("kk", "qq")
    placed = (
        P(rows, "section"),
        P(rows, "section"),
        P(rows, "section"),
        P(rows, "section"),
        P(rows, "section"),
        P(rows, "section"),
        P(),
        P("section", rows, None),
    )
    return jax.shard_map(
        body,
        mesh=grid,
        in_specs=placed,
        out_specs=(P(rows, "section", None), P(rows, "section")),
        check_vma=False,
    )
```

```python
import jax
import jax.numpy as jnp
from jax import lax
from jax.experimental import pallas as pl
from jax.experimental.pallas import tpu as pltpu
from jax.sharding import Mesh, PartitionSpec as P

BLOCK = 128
QUERY_GROUP = 4


def normed(values, gain, heads):
    rows = values.shape[0]
    floats = values.astype(jnp.float32).reshape(rows, heads, gain.shape[0])
    power = jnp.mean(floats * floats, axis=-1, keepdims=True)
    return (floats * lax.rsqrt(power + 1e-06) * gain).astype(jnp.bfloat16)


def attend_kernel(qi_ref, qt_ref, ki_ref, kt_ref, vi_ref, vt_ref, fl_ref, ni_ref, nt_ref, di_ref, dt_ref):
    head_size = qi_ref.shape[-1]
    scale = head_size ** (-0.5)
    q_blocks = qi_ref.shape[0]
    dims = (((1,), (1,)), ((), ()))
    keys_img = ki_ref[0].reshape(-1, head_size)
    keys_txt = kt_ref[...]
    vals_img = vi_ref[0].reshape(-1, head_size)
    vals_txt = vt_ref[...]

    def one(q, flags):
        s_img = lax.dot_general(q, keys_img, dims, preferred_element_type=jnp.float32) * scale
        s_txt = lax.dot_general(q, keys_txt, dims, preferred_element_type=jnp.float32) * scale
        e_img = jnp.exp(s_img)
        if flags is not None:
            e_img = jnp.where(flags > 0, e_img, jnp.float32(0.0))
        e_txt = jnp.exp(s_txt)
        den = jnp.sum(e_img, axis=1, keepdims=True) + jnp.sum(e_txt, axis=1, keepdims=True)
        num = jnp.dot(e_img.astype(jnp.bfloat16), vals_img, preferred_element_type=jnp.float32)
        num = num + jnp.dot(e_txt.astype(jnp.bfloat16), vals_txt, preferred_element_type=jnp.float32)
        return num, den

    for a in range(q_blocks):
        rows = slice(a * BLOCK, (a + 1) * BLOCK)
        num, den = one(qi_ref[a], fl_ref[0, a:a + 1, :])
        ni_ref[rows, :] = num
        di_ref[rows, :] = jnp.broadcast_to(den, num.shape)
    num, den = one(qt_ref[...], None)
    nt_ref[...] = num
    dt_ref[...] = jnp.broadcast_to(den, num.shape)


def attend(qi, qt, kv, kt, vt, fl, heads, head_size):
    groups_q = qi.shape[0]
    groups_k = kv.shape[1]
    n_qi = groups_q * BLOCK
    n_ki = groups_k * BLOCK
    n_qt, n_kt = qt.shape[0], kt.shape[0]
    width = heads * head_size

    def cols(rows):
        return pl.BlockSpec((rows, head_size), lambda h: (0, h))

    return pl.pallas_call(
        attend_kernel,
        grid=(heads,),
        in_specs=[
            pl.BlockSpec((groups_q, BLOCK, head_size), lambda h: (0, 0, h)),
            cols(n_qt),
            pl.BlockSpec((1, groups_k, BLOCK, head_size), lambda h: (0, 0, 0, h)),
            cols(n_kt),
            pl.BlockSpec((1, groups_k, BLOCK, head_size), lambda h: (1, 0, 0, h)),
            cols(n_kt),
            pl.BlockSpec((1,) + fl.shape[1:], lambda h: (h, 0, 0)),
        ],
        out_specs=[cols(n_qi), cols(n_qt), cols(n_qi), cols(n_qt)],
        out_shape=[
            jax.ShapeDtypeStruct((n_qi, width), jnp.float32),
            jax.ShapeDtypeStruct((n_qt, width), jnp.float32),
            jax.ShapeDtypeStruct((n_qi, width), jnp.float32),
            jax.ShapeDtypeStruct((n_qt, width), jnp.float32),
        ],
        compiler_params=pltpu.CompilerParams(vmem_limit_bytes=48 * 1024 * 1024),
    )(qi, qt, kv, kt, kv, vt, fl)


def body(q_img, k_img, v_img, q_txt, k_txt, v_txt, norm_gains, block_map):
    rows, width = q_img.shape
    head_size = norm_gains.shape[1]
    heads = width // head_size
    text_rows = q_txt.shape[0]
    stride = rows + text_rows
    groups_q = lax.axis_size("qq")
    groups_k = lax.axis_size("kk")
    own_q = lax.axis_index("qq")

    queries = jnp.concatenate(
        [normed(q_img, norm_gains[0], heads), normed(q_txt, norm_gains[2], heads)], axis=0
    ).reshape(1, stride, width)
    keys = jnp.concatenate(
        [normed(k_img, norm_gains[1], heads), normed(k_txt, norm_gains[3], heads)], axis=0
    ).reshape(1, stride, width)
    values = jnp.concatenate([v_img, v_txt], axis=0).reshape(1, stride, width)
    pair = jnp.stack([keys, values], axis=0)

    all_q = lax.all_gather(queries, "qq", axis=0, tiled=True)
    all_kv = lax.all_gather(pair, "kk", axis=1, tiled=True)
    flags = lax.all_gather(block_map, "qq", axis=1, tiled=True)
    flags = flags.reshape(heads, groups_q, groups_k, groups_q)
    flags = lax.dynamic_index_in_dim(flags, own_q, axis=3, keepdims=False)
    flags = jnp.repeat(flags, BLOCK, axis=2)

    qt = all_q[:, rows:].reshape(groups_q * text_rows, width)
    kt = all_kv[0, :, rows:].reshape(groups_k * text_rows, width)
    vt = all_kv[1, :, rows:].reshape(groups_k * text_rows, width)

    ni, nt, di, dt = attend(all_q, qt, all_kv, kt, vt, flags, heads, head_size)
    numer = jnp.concatenate(
        [ni.reshape(groups_q, rows, width), nt.reshape(groups_q, text_rows, width)], axis=1
    )
    denom = jnp.concatenate(
        [di[:, ::head_size].reshape(groups_q, rows, heads),
         dt[:, ::head_size].reshape(groups_q, text_rows, heads)], axis=1
    )
    denom_hi = denom.astype(jnp.bfloat16)
    denom_lo = (denom - denom_hi.astype(jnp.float32)).astype(jnp.bfloat16)
    packed = jnp.concatenate([numer.astype(jnp.bfloat16), denom_hi, denom_lo], axis=2)
    packed = lax.all_to_all(packed, "qq", split_axis=0, concat_axis=0, tiled=True)
    packed = jnp.sum(packed.astype(jnp.float32), axis=0)
    numer = packed[:, :width].reshape(stride, heads, head_size)
    denom = packed[:, width:width + heads] + packed[:, width + heads:]
    result = numer / denom[..., None]
    merged = result.reshape(stride, width).astype(jnp.bfloat16)
    image_part = merged[:rows]
    text_out = merged[rows:]
    sections = lax.axis_size("section")
    image_out = lax.all_to_all(
        image_part.reshape(rows // sections, sections, width),
        "section",
        split_axis=1,
        concat_axis=2,
        tiled=True,
    )
    return (image_out, text_out)


def solution(mesh):
    sections, seq = mesh.devices.shape
    grid = Mesh(
        mesh.devices.reshape(sections, seq // QUERY_GROUP, QUERY_GROUP),
        ("section", "kk", "qq"),
    )
    rows = ("kk", "qq")
    placed = (
        P(rows, "section"),
        P(rows, "section"),
        P(rows, "section"),
        P(rows, "section"),
        P(rows, "section"),
        P(rows, "section"),
        P(),
        P("section", rows, None),
    )
    return jax.shard_map(
        body,
        mesh=grid,
        in_specs=placed,
        out_specs=(P(rows, "section", None), P(rows, "section")),
        check_vma=False,
    )
```

```python
import jax
import jax.numpy as jnp
from jax import lax
from jax.experimental import pallas as pl
from jax.experimental.pallas import tpu as pltpu
from jax.sharding import Mesh, PartitionSpec as P

BLOCK = 128
QUERY_GROUP = 4
CHUNKS = 3


def normed(values, gain, heads):
    rows = values.shape[0]
    floats = values.astype(jnp.float32).reshape(rows, heads, gain.shape[0])
    power = jnp.mean(floats * floats, axis=-1, keepdims=True)
    return (floats * lax.rsqrt(power + 1e-06) * gain).astype(jnp.bfloat16)


def attend_kernel(qi_ref, qt_ref, ki_ref, kt_ref, vi_ref, vt_ref, fl_ref, ni_ref, nt_ref, di_ref, dt_ref):
    head_size = qi_ref.shape[-1]
    scale = head_size ** (-0.5)
    q_blocks = qi_ref.shape[0]
    dims = (((1,), (1,)), ((), ()))
    keys_img = ki_ref[0].reshape(-1, head_size)
    keys_txt = kt_ref[...]
    vals_img = vi_ref[0].reshape(-1, head_size)
    vals_txt = vt_ref[...]

    def one(q, flags):
        s_img = lax.dot_general(q, keys_img, dims, preferred_element_type=jnp.float32) * scale
        s_txt = lax.dot_general(q, keys_txt, dims, preferred_element_type=jnp.float32) * scale
        e_img = jnp.exp(s_img)
        if flags is not None:
            e_img = jnp.where(flags > 0, e_img, jnp.float32(0.0))
        e_txt = jnp.exp(s_txt)
        den = jnp.sum(e_img, axis=1, keepdims=True) + jnp.sum(e_txt, axis=1, keepdims=True)
        num = jnp.dot(e_img.astype(jnp.bfloat16), vals_img, preferred_element_type=jnp.float32)
        num = num + jnp.dot(e_txt.astype(jnp.bfloat16), vals_txt, preferred_element_type=jnp.float32)
        return num, den

    for a in range(q_blocks):
        rows = slice(a * BLOCK, (a + 1) * BLOCK)
        num, den = one(qi_ref[a], fl_ref[0, a:a + 1, :])
        ni_ref[rows, :] = num
        di_ref[rows, :] = jnp.broadcast_to(den, num.shape)
    num, den = one(qt_ref[...], None)
    nt_ref[...] = num
    dt_ref[...] = jnp.broadcast_to(den, num.shape)


def attend(qi, qt, kv, kt, vt, fl, first, heads, head_size):
    groups_q = qi.shape[0]
    groups_k = kv.shape[1]
    n_qi = groups_q * BLOCK
    n_qt, n_kt = qt.shape[0], kt.shape[0]
    width = heads * head_size

    def cols(rows, offset=0):
        return pl.BlockSpec((rows, head_size), lambda h: (0, h + offset))

    return pl.pallas_call(
        attend_kernel,
        grid=(heads,),
        in_specs=[
            pl.BlockSpec((groups_q, BLOCK, head_size), lambda h: (0, 0, h + first)),
            cols(n_qt, first),
            pl.BlockSpec((1, groups_k, BLOCK, head_size), lambda h: (0, 0, 0, h)),
            cols(n_kt),
            pl.BlockSpec((1, groups_k, BLOCK, head_size), lambda h: (1, 0, 0, h)),
            cols(n_kt),
            pl.BlockSpec((1,) + fl.shape[1:], lambda h: (h + first, 0, 0)),
        ],
        out_specs=[cols(n_qi), cols(n_qt), cols(n_qi), cols(n_qt)],
        out_shape=[
            jax.ShapeDtypeStruct((n_qi, width), jnp.float32),
            jax.ShapeDtypeStruct((n_qt, width), jnp.float32),
            jax.ShapeDtypeStruct((n_qi, width), jnp.float32),
            jax.ShapeDtypeStruct((n_qt, width), jnp.float32),
        ],
        compiler_params=pltpu.CompilerParams(vmem_limit_bytes=48 * 1024 * 1024),
    )(qi, qt, kv, kt, kv, vt, fl)


def body(q_img, k_img, v_img, q_txt, k_txt, v_txt, norm_gains, block_map):
    rows, width = q_img.shape
    head_size = norm_gains.shape[1]
    heads = width // head_size
    text_rows = q_txt.shape[0]
    stride = rows + text_rows
    groups_q = lax.axis_size("qq")
    groups_k = lax.axis_size("kk")
    own_q = lax.axis_index("qq")
    sections = lax.axis_size("section")
    chunk = heads // CHUNKS

    map_row = block_map.reshape(1, -1).astype(jnp.bfloat16)
    map_row = jnp.pad(map_row, ((0, 0), (0, width - map_row.shape[1])))
    queries = jnp.concatenate(
        [normed(q_img, norm_gains[0], heads).reshape(rows, width),
         normed(q_txt, norm_gains[2], heads).reshape(text_rows, width),
         map_row], axis=0
    ).reshape(1, stride + 1, width)
    keys = jnp.concatenate(
        [normed(k_img, norm_gains[1], heads), normed(k_txt, norm_gains[3], heads)], axis=0
    ).reshape(1, stride, width)
    values = jnp.concatenate([v_img, v_txt], axis=0).reshape(1, stride, width)
    pair = jnp.stack([keys, values], axis=0)

    all_q = lax.all_gather(queries, "qq", axis=0, tiled=True)
    flags = all_q[:, stride, :block_map.size].reshape(groups_q, heads, groups_k, groups_q)
    flags = lax.dynamic_index_in_dim(flags, own_q, axis=3, keepdims=False)
    flags = jnp.repeat(flags.transpose(1, 0, 2), BLOCK, axis=2)
    qt = all_q[:, rows:stride].reshape(groups_q * text_rows, width)

    image_parts = []
    text_parts = []
    for c in range(CHUNKS):
        span = slice(c * chunk * head_size, (c + 1) * chunk * head_size)
        all_kv = lax.all_gather(pair[..., span], "kk", axis=1, tiled=True)
        kt = all_kv[0, :, rows:].reshape(groups_k * text_rows, chunk * head_size)
        vt = all_kv[1, :, rows:].reshape(groups_k * text_rows, chunk * head_size)
        ni, nt, di, dt = attend(all_q, qt, all_kv, kt, vt, flags, c * chunk, chunk, head_size)
        numer = jnp.concatenate(
            [ni.reshape(groups_q, rows, -1), nt.reshape(groups_q, text_rows, -1)], axis=1
        )
        denom = jnp.concatenate(
            [di[:, ::head_size].reshape(groups_q, rows, chunk),
             dt[:, ::head_size].reshape(groups_q, text_rows, chunk)], axis=1
        )
        denom_hi = denom.astype(jnp.bfloat16)
        denom_lo = (denom - denom_hi.astype(jnp.float32)).astype(jnp.bfloat16)
        packed = jnp.concatenate([numer.astype(jnp.bfloat16), denom_hi, denom_lo], axis=2)
        packed = lax.all_to_all(packed, "qq", split_axis=0, concat_axis=0, tiled=True)
        packed = jnp.sum(packed.astype(jnp.float32), axis=0)
        part_width = chunk * head_size
        numer = packed[:, :part_width].reshape(stride, chunk, head_size)
        denom = packed[:, part_width:part_width + chunk] + packed[:, part_width + chunk:]
        result = numer / denom[..., None]
        merged = result.reshape(stride, part_width).astype(jnp.bfloat16)
        text_parts.append(merged[rows:])
        image_part = lax.all_to_all(
            merged[:rows].reshape(rows // sections, sections, part_width),
            "section",
            split_axis=1,
            concat_axis=2,
            tiled=True,
        )
        image_parts.append(image_part.reshape(rows // sections, 1, sections, part_width))
    image_out = jnp.stack(image_parts, axis=3).reshape(rows // sections, 1, sections * width)
    text_out = jnp.concatenate(text_parts, axis=1)
    return (image_out, text_out)


def solution(mesh):
    sections, seq = mesh.devices.shape
    grid = Mesh(
        mesh.devices.reshape(sections, seq // QUERY_GROUP, QUERY_GROUP),
        ("section", "kk", "qq"),
    )
    rows = ("kk", "qq")
    placed = (
        P(rows, "section"),
        P(rows, "section"),
        P(rows, "section"),
        P(rows, "section"),
        P(rows, "section"),
        P(rows, "section"),
        P(),
        P("section", rows, None),
    )
    return jax.shard_map(
        body,
        mesh=grid,
        in_specs=placed,
        out_specs=(P(rows, "section", None), P(rows, "section")),
        check_vma=False,
    )
```

```python
import jax
import jax.numpy as jnp
from jax import lax
from jax.experimental import pallas as pl
from jax.experimental.pallas import tpu as pltpu
from jax.sharding import Mesh, PartitionSpec as P

BLOCK = 128
SIDE = 4
QUERY_AXES = "x"
KEY_AXES = ("y", "zh")


def normed(values, gain, heads):
    rows = values.shape[0]
    floats = values.astype(jnp.float32).reshape(rows, heads, gain.shape[0])
    power = jnp.mean(floats * floats, axis=-1, keepdims=True)
    return (floats * lax.rsqrt(power + 1e-06) * gain).astype(jnp.bfloat16)


def attend_kernel(qi_ref, qt_ref, ki_ref, kt_ref, vi_ref, vt_ref, fl_ref, ni_ref, nt_ref, di_ref, dt_ref):
    head_size = qi_ref.shape[-1]
    scale = head_size ** (-0.5)
    q_blocks = qi_ref.shape[0]
    dims = (((1,), (1,)), ((), ()))
    keys_img = ki_ref[0].reshape(-1, head_size)
    keys_txt = kt_ref[...]
    vals_img = vi_ref[0].reshape(-1, head_size)
    vals_txt = vt_ref[...]

    def one(q, flags):
        s_img = lax.dot_general(q, keys_img, dims, preferred_element_type=jnp.float32) * scale
        s_txt = lax.dot_general(q, keys_txt, dims, preferred_element_type=jnp.float32) * scale
        e_img = jnp.exp(s_img)
        if flags is not None:
            e_img = jnp.where(flags > 0, e_img, jnp.float32(0.0))
        e_txt = jnp.exp(s_txt)
        den = jnp.sum(e_img, axis=1, keepdims=True) + jnp.sum(e_txt, axis=1, keepdims=True)
        num = jnp.dot(e_img.astype(jnp.bfloat16), vals_img, preferred_element_type=jnp.float32)
        num = num + jnp.dot(e_txt.astype(jnp.bfloat16), vals_txt, preferred_element_type=jnp.float32)
        return num, den

    for a in range(q_blocks):
        rows = slice(a * BLOCK, (a + 1) * BLOCK)
        num, den = one(qi_ref[a], fl_ref[0, a:a + 1, :])
        ni_ref[rows, :] = num
        di_ref[rows, :] = jnp.broadcast_to(den, num.shape)
    num, den = one(qt_ref[...], None)
    nt_ref[...] = num
    dt_ref[...] = jnp.broadcast_to(den, num.shape)


def attend(qi, qt, kv, kt, vt, fl, heads, head_size):
    groups_q = qi.shape[0]
    groups_k = kv.shape[1]
    n_qi = groups_q * BLOCK
    n_ki = groups_k * BLOCK
    n_qt, n_kt = qt.shape[0], kt.shape[0]
    width = heads * head_size

    def cols(rows):
        return pl.BlockSpec((rows, head_size), lambda h: (0, h))

    return pl.pallas_call(
        attend_kernel,
        grid=(heads,),
        in_specs=[
            pl.BlockSpec((groups_q, BLOCK, head_size), lambda h: (0, 0, h)),
            cols(n_qt),
            pl.BlockSpec((1, groups_k, BLOCK, head_size), lambda h: (0, 0, 0, h)),
            cols(n_kt),
            pl.BlockSpec((1, groups_k, BLOCK, head_size), lambda h: (1, 0, 0, h)),
            cols(n_kt),
            pl.BlockSpec((1,) + fl.shape[1:], lambda h: (h, 0, 0)),
        ],
        out_specs=[cols(n_qi), cols(n_qt), cols(n_qi), cols(n_qt)],
        out_shape=[
            jax.ShapeDtypeStruct((n_qi, width), jnp.float32),
            jax.ShapeDtypeStruct((n_qt, width), jnp.float32),
            jax.ShapeDtypeStruct((n_qi, width), jnp.float32),
            jax.ShapeDtypeStruct((n_qt, width), jnp.float32),
        ],
        compiler_params=pltpu.CompilerParams(vmem_limit_bytes=48 * 1024 * 1024),
    )(qi, qt, kv, kt, kv, vt, fl)


def body(q_img, k_img, v_img, q_txt, k_txt, v_txt, norm_gains, block_map):
    rows, width = q_img.shape
    head_size = norm_gains.shape[1]
    heads = width // head_size
    text_rows = q_txt.shape[0]
    stride = rows + text_rows
    groups_q = lax.axis_size(QUERY_AXES)
    groups_k = lax.axis_size(KEY_AXES)
    own_x = lax.axis_index("x")
    size_x = lax.axis_size("x")
    size_y = lax.axis_size("y")

    map_row = block_map.reshape(1, -1).astype(jnp.bfloat16)
    map_row = jnp.pad(map_row, ((0, 0), (0, width - map_row.shape[1])))
    queries = jnp.concatenate(
        [normed(q_img, norm_gains[0], heads).reshape(rows, width),
         normed(q_txt, norm_gains[2], heads).reshape(text_rows, width),
         map_row], axis=0
    ).reshape(1, stride + 1, width)
    keys = jnp.concatenate(
        [normed(k_img, norm_gains[1], heads), normed(k_txt, norm_gains[3], heads)], axis=0
    ).reshape(1, stride, width)
    values = jnp.concatenate([v_img, v_txt], axis=0).reshape(1, stride, width)
    pair = jnp.stack([keys, values], axis=0)

    all_q = lax.all_gather(queries, QUERY_AXES, axis=0, tiled=True)
    all_kv = lax.all_gather(pair, KEY_AXES, axis=1, tiled=True)
    flags = all_q[:, stride, :block_map.size].reshape(groups_q, heads, size_y, size_x, -1)
    flags = lax.dynamic_index_in_dim(flags, own_x, axis=3, keepdims=False)
    flags = flags.reshape(groups_q, heads, groups_k).transpose(1, 0, 2)
    flags = jnp.repeat(flags, BLOCK, axis=2)

    qt = all_q[:, rows:stride].reshape(groups_q * text_rows, width)
    kt = all_kv[0, :, rows:].reshape(groups_k * text_rows, width)
    vt = all_kv[1, :, rows:].reshape(groups_k * text_rows, width)

    ni, nt, di, dt = attend(all_q, qt, all_kv, kt, vt, flags, heads, head_size)
    numer = jnp.concatenate(
        [ni.reshape(groups_q, rows, width), nt.reshape(groups_q, text_rows, width)], axis=1
    )
    denom = jnp.concatenate(
        [di[:, ::head_size].reshape(groups_q, rows, heads),
         dt[:, ::head_size].reshape(groups_q, text_rows, heads)], axis=1
    )
    denom_hi = denom.astype(jnp.bfloat16)
    denom_lo = (denom - denom_hi.astype(jnp.float32)).astype(jnp.bfloat16)
    packed = jnp.concatenate([numer.astype(jnp.bfloat16), denom_hi, denom_lo], axis=2)
    packed = lax.all_to_all(packed, QUERY_AXES, split_axis=0, concat_axis=0, tiled=True)
    packed = jnp.sum(packed.astype(jnp.float32), axis=0)
    numer = packed[:, :width].reshape(stride, heads, head_size)
    denom = packed[:, width:width + heads] + packed[:, width + heads:]
    result = numer / denom[..., None]
    merged = result.reshape(stride, width).astype(jnp.bfloat16)
    image_part = merged[:rows]
    text_out = merged[rows:]
    sections = lax.axis_size("section")
    image_out = lax.all_to_all(
        image_part.reshape(rows // sections, sections, width),
        "section",
        split_axis=1,
        concat_axis=2,
        tiled=True,
    )
    return (image_out, text_out)


def solution(mesh):
    sections, seq = mesh.devices.shape
    grid = Mesh(
        mesh.devices.reshape(sections, seq // (SIDE * SIDE), SIDE, SIDE),
        ("section", "y", "x", "zh"),
    )
    rows = ("y", "x", "zh")
    placed = (
        P(rows, "section"),
        P(rows, "section"),
        P(rows, "section"),
        P(rows, "section"),
        P(rows, "section"),
        P(rows, "section"),
        P(),
        P("section", rows, None),
    )
    return jax.shard_map(
        body,
        mesh=grid,
        in_specs=placed,
        out_specs=(P(rows, "section", None), P(rows, "section")),
        check_vma=False,
    )
```

```python
import jax
import jax.numpy as jnp
from jax import lax
from jax.experimental import pallas as pl
from jax.experimental.pallas import tpu as pltpu
from jax.sharding import Mesh, PartitionSpec as P

BLOCK = 128
SIDE = 4
QUERY_AXES = ("x_lo", "zh")
KEY_AXES = ("y", "x_hi")


def normed(values, gain, heads):
    rows = values.shape[0]
    floats = values.astype(jnp.float32).reshape(rows, heads, gain.shape[0])
    power = jnp.mean(floats * floats, axis=-1, keepdims=True)
    return (floats * lax.rsqrt(power + 1e-06) * gain).astype(jnp.bfloat16)


def attend_kernel(qi_ref, qt_ref, ki_ref, kt_ref, vi_ref, vt_ref, fl_ref, ni_ref, nt_ref, di_ref, dt_ref):
    head_size = qi_ref.shape[-1]
    scale = head_size ** (-0.5)
    q_blocks = qi_ref.shape[0]
    dims = (((1,), (1,)), ((), ()))
    keys_img = ki_ref[0].reshape(-1, head_size)
    keys_txt = kt_ref[...]
    vals_img = vi_ref[0].reshape(-1, head_size)
    vals_txt = vt_ref[...]

    def one(q, flags):
        s_img = lax.dot_general(q, keys_img, dims, preferred_element_type=jnp.float32) * scale
        s_txt = lax.dot_general(q, keys_txt, dims, preferred_element_type=jnp.float32) * scale
        e_img = jnp.exp(s_img)
        if flags is not None:
            e_img = jnp.where(flags > 0, e_img, jnp.float32(0.0))
        e_txt = jnp.exp(s_txt)
        den = jnp.sum(e_img, axis=1, keepdims=True) + jnp.sum(e_txt, axis=1, keepdims=True)
        num = jnp.dot(e_img.astype(jnp.bfloat16), vals_img, preferred_element_type=jnp.float32)
        num = num + jnp.dot(e_txt.astype(jnp.bfloat16), vals_txt, preferred_element_type=jnp.float32)
        return num, den

    for a in range(q_blocks):
        rows = slice(a * BLOCK, (a + 1) * BLOCK)
        num, den = one(qi_ref[a], fl_ref[0, a:a + 1, :])
        ni_ref[rows, :] = num
        di_ref[rows, :] = jnp.broadcast_to(den, num.shape)
    num, den = one(qt_ref[...], None)
    nt_ref[...] = num
    dt_ref[...] = jnp.broadcast_to(den, num.shape)


def attend(qi, qt, kv, kt, vt, fl, heads, head_size):
    groups_q = qi.shape[0]
    groups_k = kv.shape[1]
    n_qi = groups_q * BLOCK
    n_ki = groups_k * BLOCK
    n_qt, n_kt = qt.shape[0], kt.shape[0]
    width = heads * head_size

    def cols(rows):
        return pl.BlockSpec((rows, head_size), lambda h: (0, h))

    return pl.pallas_call(
        attend_kernel,
        grid=(heads,),
        in_specs=[
            pl.BlockSpec((groups_q, BLOCK, head_size), lambda h: (0, 0, h)),
            cols(n_qt),
            pl.BlockSpec((1, groups_k, BLOCK, head_size), lambda h: (0, 0, 0, h)),
            cols(n_kt),
            pl.BlockSpec((1, groups_k, BLOCK, head_size), lambda h: (1, 0, 0, h)),
            cols(n_kt),
            pl.BlockSpec((1,) + fl.shape[1:], lambda h: (h, 0, 0)),
        ],
        out_specs=[cols(n_qi), cols(n_qt), cols(n_qi), cols(n_qt)],
        out_shape=[
            jax.ShapeDtypeStruct((n_qi, width), jnp.float32),
            jax.ShapeDtypeStruct((n_qt, width), jnp.float32),
            jax.ShapeDtypeStruct((n_qi, width), jnp.float32),
            jax.ShapeDtypeStruct((n_qt, width), jnp.float32),
        ],
        compiler_params=pltpu.CompilerParams(vmem_limit_bytes=48 * 1024 * 1024),
    )(qi, qt, kv, kt, kv, vt, fl)


def body(q_img, k_img, v_img, q_txt, k_txt, v_txt, norm_gains, block_map):
    rows, width = q_img.shape
    head_size = norm_gains.shape[1]
    heads = width // head_size
    text_rows = q_txt.shape[0]
    stride = rows + text_rows
    groups_q = lax.axis_size(QUERY_AXES)
    groups_k = lax.axis_size(KEY_AXES)

    map_row = block_map.reshape(1, -1).astype(jnp.bfloat16)
    map_row = jnp.pad(map_row, ((0, 0), (0, width - map_row.shape[1])))
    queries = jnp.concatenate(
        [normed(q_img, norm_gains[0], heads).reshape(rows, width),
         normed(q_txt, norm_gains[2], heads).reshape(text_rows, width),
         map_row], axis=0
    ).reshape(1, stride + 1, width)
    keys = jnp.concatenate(
        [normed(k_img, norm_gains[1], heads), normed(k_txt, norm_gains[3], heads)], axis=0
    ).reshape(1, stride, width)
    values = jnp.concatenate([v_img, v_txt], axis=0).reshape(1, stride, width)
    pair = jnp.stack([keys, values], axis=0)

    all_q = lax.all_gather(queries, QUERY_AXES, axis=0, tiled=True)
    all_kv = lax.all_gather(pair, KEY_AXES, axis=1, tiled=True)
    seq_axes = ("y", "x_hi", "x_lo", "zh")
    flags = all_q[:, stride, :block_map.size].reshape(
        (groups_q, heads) + tuple(lax.axis_size(n) for n in seq_axes)
    )
    kept = [n for n in seq_axes]
    for name in QUERY_AXES:
        place = 2 + kept.index(name)
        flags = lax.dynamic_index_in_dim(flags, lax.axis_index(name), axis=place, keepdims=False)
        kept.remove(name)
    flags = flags.reshape(groups_q, heads, groups_k).transpose(1, 0, 2)
    flags = jnp.repeat(flags, BLOCK, axis=2)

    qt = all_q[:, rows:stride].reshape(groups_q * text_rows, width)
    kt = all_kv[0, :, rows:].reshape(groups_k * text_rows, width)
    vt = all_kv[1, :, rows:].reshape(groups_k * text_rows, width)

    ni, nt, di, dt = attend(all_q, qt, all_kv, kt, vt, flags, heads, head_size)
    numer = jnp.concatenate(
        [ni.reshape(groups_q, rows, width), nt.reshape(groups_q, text_rows, width)], axis=1
    )
    denom = jnp.concatenate(
        [di[:, ::head_size].reshape(groups_q, rows, heads),
         dt[:, ::head_size].reshape(groups_q, text_rows, heads)], axis=1
    )
    denom_hi = denom.astype(jnp.bfloat16)
    denom_lo = (denom - denom_hi.astype(jnp.float32)).astype(jnp.bfloat16)
    packed = jnp.concatenate([numer.astype(jnp.bfloat16), denom_hi, denom_lo], axis=2)
    packed = lax.all_to_all(packed, QUERY_AXES, split_axis=0, concat_axis=0, tiled=True)
    packed = jnp.sum(packed.astype(jnp.float32), axis=0)
    numer = packed[:, :width].reshape(stride, heads, head_size)
    denom = packed[:, width:width + heads] + packed[:, width + heads:]
    result = numer / denom[..., None]
    merged = result.reshape(stride, width).astype(jnp.bfloat16)
    image_part = merged[:rows]
    text_out = merged[rows:]
    sections = lax.axis_size("section")
    image_out = lax.all_to_all(
        image_part.reshape(rows // sections, sections, width),
        "section",
        split_axis=1,
        concat_axis=2,
        tiled=True,
    )
    return (image_out, text_out)


def solution(mesh):
    sections, seq = mesh.devices.shape
    side = SIDE
    grid = Mesh(
        mesh.devices.reshape(sections, seq // (side * side), 2, side // 2, side),
        ("section", "y", "x_hi", "x_lo", "zh"),
    )
    rows = ("y", "x_hi", "x_lo", "zh")
    placed = (
        P(rows, "section"),
        P(rows, "section"),
        P(rows, "section"),
        P(rows, "section"),
        P(rows, "section"),
        P(rows, "section"),
        P(),
        P("section", rows, None),
    )
    return jax.shard_map(
        body,
        mesh=grid,
        in_specs=placed,
        out_specs=(P(rows, "section", None), P(rows, "section")),
        check_vma=False,
    )
```

```python
import jax
import jax.numpy as jnp
from jax import lax
from jax.experimental import pallas as pl
from jax.experimental.pallas import tpu as pltpu
from jax.sharding import Mesh, PartitionSpec as P

BLOCK = 128
QUERY_GROUP = 4


def normed(values, gain, heads):
    rows = values.shape[0]
    floats = values.astype(jnp.float32).reshape(rows, heads, gain.shape[0])
    power = jnp.mean(floats * floats, axis=-1, keepdims=True)
    return (floats * lax.rsqrt(power + 1e-06) * gain).astype(jnp.bfloat16)


def attend_kernel(qi_ref, qt_ref, ki_ref, kt_ref, vi_ref, vt_ref, fl_ref, ni_ref, nt_ref, di_ref, dt_ref):
    head_size = qi_ref.shape[-1]
    scale = head_size ** (-0.5)
    q_blocks = qi_ref.shape[0]
    dims = (((1,), (1,)), ((), ()))
    keys_img = ki_ref[0].reshape(-1, head_size)
    keys_txt = kt_ref[...]
    vals_img = vi_ref[0].reshape(-1, head_size)
    vals_txt = vt_ref[...]

    def one(q, flags):
        s_img = lax.dot_general(q, keys_img, dims, preferred_element_type=jnp.float32) * scale
        s_txt = lax.dot_general(q, keys_txt, dims, preferred_element_type=jnp.float32) * scale
        e_img = jnp.exp(s_img)
        if flags is not None:
            e_img = jnp.where(flags > 0, e_img, jnp.float32(0.0))
        e_txt = jnp.exp(s_txt)
        den = jnp.sum(e_img, axis=1, keepdims=True) + jnp.sum(e_txt, axis=1, keepdims=True)
        num = jnp.dot(e_img.astype(jnp.bfloat16), vals_img, preferred_element_type=jnp.float32)
        num = num + jnp.dot(e_txt.astype(jnp.bfloat16), vals_txt, preferred_element_type=jnp.float32)
        return num, den

    for a in range(q_blocks):
        rows = slice(a * BLOCK, (a + 1) * BLOCK)
        num, den = one(qi_ref[a], fl_ref[0, a:a + 1, :])
        ni_ref[rows, :] = num
        di_ref[rows, :] = jnp.broadcast_to(den, num.shape)
    num, den = one(qt_ref[...], None)
    nt_ref[...] = num
    dt_ref[...] = jnp.broadcast_to(den, num.shape)


def attend(qi, qt, kv, kt, vt, fl, heads, head_size):
    groups_q = qi.shape[0]
    groups_k = kv.shape[1]
    n_qi = groups_q * BLOCK
    n_ki = groups_k * BLOCK
    n_qt, n_kt = qt.shape[0], kt.shape[0]
    width = heads * head_size

    def cols(rows):
        return pl.BlockSpec((rows, head_size), lambda h: (0, h))

    return pl.pallas_call(
        attend_kernel,
        grid=(heads,),
        in_specs=[
            pl.BlockSpec((groups_q, BLOCK, head_size), lambda h: (0, 0, h)),
            cols(n_qt),
            pl.BlockSpec((1, groups_k, BLOCK, head_size), lambda h: (0, 0, 0, h)),
            cols(n_kt),
            pl.BlockSpec((1, groups_k, BLOCK, head_size), lambda h: (1, 0, 0, h)),
            cols(n_kt),
            pl.BlockSpec((1,) + fl.shape[1:], lambda h: (h, 0, 0)),
        ],
        out_specs=[cols(n_qi), cols(n_qt), cols(n_qi), cols(n_qt)],
        out_shape=[
            jax.ShapeDtypeStruct((n_qi, width), jnp.float32),
            jax.ShapeDtypeStruct((n_qt, width), jnp.float32),
            jax.ShapeDtypeStruct((n_qi, width), jnp.float32),
            jax.ShapeDtypeStruct((n_qt, width), jnp.float32),
        ],
        compiler_params=pltpu.CompilerParams(vmem_limit_bytes=48 * 1024 * 1024),
    )(qi, qt, kv, kt, kv, vt, fl)


def body(q_img, k_img, v_img, q_txt, k_txt, v_txt, norm_gains, block_map):
    rows, width = q_img.shape
    head_size = norm_gains.shape[1]
    heads = width // head_size
    text_rows = q_txt.shape[0]
    stride = rows + text_rows
    groups_q = lax.axis_size("qq")
    groups_k = lax.axis_size("kk")
    own_q = lax.axis_index("qq")

    queries = jnp.concatenate(
        [normed(q_img, norm_gains[0], heads), normed(q_txt, norm_gains[2], heads)], axis=0
    ).reshape(1, stride, width)
    keys = jnp.concatenate(
        [normed(k_img, norm_gains[1], heads), normed(k_txt, norm_gains[3], heads)], axis=0
    ).reshape(1, stride, width)
    values = jnp.concatenate([v_img, v_txt], axis=0).reshape(1, stride, width)
    pair = jnp.stack([keys, values], axis=0)

    all_q = lax.all_gather(queries, "qq", axis=0, tiled=True)
    all_kv = lax.all_gather(pair, "kk", axis=1, tiled=True)
    flags = lax.all_gather(block_map, "qq", axis=1, tiled=True)
    flags = flags.reshape(heads, groups_q, groups_k, groups_q)
    flags = lax.dynamic_index_in_dim(flags, own_q, axis=3, keepdims=False)
    flags = jnp.repeat(flags, BLOCK, axis=2)

    qt = all_q[:, rows:].reshape(groups_q * text_rows, width)
    kt = all_kv[0, :, rows:].reshape(groups_k * text_rows, width)
    vt = all_kv[1, :, rows:].reshape(groups_k * text_rows, width)

    ni, nt, di, dt = attend(all_q, qt, all_kv, kt, vt, flags, heads, head_size)
    numer = jnp.concatenate(
        [ni.reshape(groups_q, rows, width), nt.reshape(groups_q, text_rows, width)], axis=1
    )
    denom = jnp.concatenate(
        [di[:, ::head_size].reshape(groups_q, rows, heads),
         dt[:, ::head_size].reshape(groups_q, text_rows, heads)], axis=1
    )
    denom_hi = denom.astype(jnp.bfloat16)
    denom_lo = (denom - denom_hi.astype(jnp.float32)).astype(jnp.bfloat16)
    packed = jnp.concatenate([numer.astype(jnp.bfloat16), denom_hi, denom_lo], axis=2)
    sections = lax.axis_size("section")
    per = rows // sections
    lanes = packed.shape[2]
    image_rows = packed[:, :rows].reshape(groups_q, per, sections, lanes).transpose(2, 0, 1, 3)
    text_part = jnp.broadcast_to(packed[None, :, rows:], (sections, groups_q, text_rows, lanes))
    packed = jnp.concatenate([image_rows, text_part], axis=2)
    packed = packed.reshape(sections * groups_q, per + text_rows, lanes)
    packed = lax.all_to_all(packed, ("section", "qq"), split_axis=0, concat_axis=0, tiled=True)
    packed = packed.reshape(sections, groups_q, per + text_rows, lanes)
    packed = jnp.sum(packed.astype(jnp.float32), axis=1)
    numer = packed[:, :, :width].reshape(sections, per + text_rows, heads, head_size)
    denom = packed[:, :, width:width + heads] + packed[:, :, width + heads:]
    result = (numer / denom[..., None]).astype(jnp.bfloat16)
    image_out = result[:, :per].reshape(sections, per, width).transpose(1, 0, 2)
    image_out = image_out.reshape(per, 1, sections * width)
    own_section = lax.axis_index("section")
    text_out = lax.dynamic_index_in_dim(result[:, per:], own_section, axis=0, keepdims=False)
    text_out = text_out.reshape(text_rows, width)
    return (image_out, text_out)


def solution(mesh):
    sections, seq = mesh.devices.shape
    grid = Mesh(
        mesh.devices.reshape(sections, seq // QUERY_GROUP, QUERY_GROUP),
        ("section", "kk", "qq"),
    )
    rows = ("kk", "qq")
    placed = (
        P(rows, "section"),
        P(rows, "section"),
        P(rows, "section"),
        P(rows, "section"),
        P(rows, "section"),
        P(rows, "section"),
        P(),
        P("section", rows, None),
    )
    return jax.shard_map(
        body,
        mesh=grid,
        in_specs=placed,
        out_specs=(P(rows, "section", None), P(rows, "section")),
        check_vma=False,
    )
```

```python
import jax
import jax.numpy as jnp
from jax import lax
from jax.experimental import pallas as pl
from jax.experimental.pallas import tpu as pltpu
from jax.sharding import Mesh, PartitionSpec as P

BLOCK = 128
QUERY_GROUP = 4


def normed(values, gain, heads):
    rows = values.shape[0]
    floats = values.astype(jnp.float32).reshape(rows, heads, gain.shape[0])
    power = jnp.mean(floats * floats, axis=-1, keepdims=True)
    return (floats * lax.rsqrt(power + 1e-06) * gain).astype(jnp.bfloat16)


def attend_kernel(q_ref, qt_ref, ki_ref, kt_ref, vi_ref, vt_ref, fl_ref, num_ref, den_ref):
    head = pl.program_id(0)
    head_size = q_ref.shape[-1]
    scale = head_size ** (-0.5)
    q_blocks = q_ref.shape[0]
    text_rows = qt_ref.shape[0] // q_blocks
    dims = (((1,), (1,)), ((), ()))
    keys_img = ki_ref[0].reshape(-1, head_size)
    keys_txt = kt_ref[...]
    vals_img = vi_ref[0].reshape(-1, head_size)
    vals_txt = vt_ref[...]

    @pl.when(head == 0)
    def _():
        den_ref[...] = jnp.zeros(den_ref.shape, den_ref.dtype)

    def one(q, flags):
        s_img = lax.dot_general(q, keys_img, dims, preferred_element_type=jnp.float32) * scale
        s_txt = lax.dot_general(q, keys_txt, dims, preferred_element_type=jnp.float32) * scale
        e_img = jnp.exp(s_img)
        if flags is not None:
            e_img = jnp.where(flags > 0, e_img, jnp.float32(0.0))
        e_txt = jnp.exp(s_txt)
        den = jnp.sum(e_img, axis=1, keepdims=True) + jnp.sum(e_txt, axis=1, keepdims=True)
        num = jnp.dot(e_img.astype(jnp.bfloat16), vals_img, preferred_element_type=jnp.float32)
        num = num + jnp.dot(e_txt.astype(jnp.bfloat16), vals_txt, preferred_element_type=jnp.float32)
        return num, den

    def put(a, lo, hi, num, den):
        num_ref[a, lo:hi, :] = num
        lane = lax.broadcasted_iota(jnp.int32, (hi - lo, den_ref.shape[-1]), 1)
        den_ref[a, lo:hi, :] = jnp.where(lane == head, den, den_ref[a, lo:hi, :])

    for a in range(q_blocks):
        num, den = one(q_ref[a, 0:BLOCK, :], fl_ref[0, a:a + 1, :])
        put(a, 0, BLOCK, num, den)
    num, den = one(qt_ref[...], None)
    for a in range(q_blocks):
        part = slice(a * text_rows, (a + 1) * text_rows)
        put(a, BLOCK, BLOCK + text_rows, num[part], den[part])


def attend(all_q, qt, kv, kt, vt, fl, heads, head_size):
    groups_q, stride = all_q.shape[0], all_q.shape[1]
    groups_k = kv.shape[1]
    n_qt, n_kt = qt.shape[0], kt.shape[0]
    width = heads * head_size

    def cols(rows):
        return pl.BlockSpec((rows, head_size), lambda h: (0, h))

    return pl.pallas_call(
        attend_kernel,
        grid=(heads,),
        in_specs=[
            pl.BlockSpec((groups_q, stride, head_size), lambda h: (0, 0, h)),
            cols(n_qt),
            pl.BlockSpec((1, groups_k, BLOCK, head_size), lambda h: (0, 0, 0, h)),
            cols(n_kt),
            pl.BlockSpec((1, groups_k, BLOCK, head_size), lambda h: (1, 0, 0, h)),
            cols(n_kt),
            pl.BlockSpec((1,) + fl.shape[1:], lambda h: (h, 0, 0)),
        ],
        out_specs=[
            pl.BlockSpec((groups_q, stride, head_size), lambda h: (0, 0, h)),
            pl.BlockSpec((groups_q, stride, BLOCK), lambda h: (0, 0, 0)),
        ],
        out_shape=[
            jax.ShapeDtypeStruct((groups_q, stride, width), jnp.float32),
            jax.ShapeDtypeStruct((groups_q, stride, BLOCK), jnp.float32),
        ],
        compiler_params=pltpu.CompilerParams(vmem_limit_bytes=48 * 1024 * 1024),
    )(all_q, qt, kv, kt, kv, vt, fl)


def body(q_img, k_img, v_img, q_txt, k_txt, v_txt, norm_gains, block_map):
    rows, width = q_img.shape
    head_size = norm_gains.shape[1]
    heads = width // head_size
    text_rows = q_txt.shape[0]
    stride = rows + text_rows
    groups_q = lax.axis_size("qq")
    groups_k = lax.axis_size("kk")
    own_q = lax.axis_index("qq")

    queries = jnp.concatenate(
        [normed(q_img, norm_gains[0], heads), normed(q_txt, norm_gains[2], heads)], axis=0
    ).reshape(1, stride, width)
    keys = jnp.concatenate(
        [normed(k_img, norm_gains[1], heads), normed(k_txt, norm_gains[3], heads)], axis=0
    ).reshape(1, stride, width)
    values = jnp.concatenate([v_img, v_txt], axis=0).reshape(1, stride, width)
    pair = jnp.stack([keys, values], axis=0)

    all_q = lax.all_gather(queries, "qq", axis=0, tiled=True)
    all_kv = lax.all_gather(pair, "kk", axis=1, tiled=True)
    flags = lax.all_gather(block_map, "qq", axis=1, tiled=True)
    flags = flags.reshape(heads, groups_q, groups_k, groups_q)
    flags = lax.dynamic_index_in_dim(flags, own_q, axis=3, keepdims=False)
    flags = jnp.repeat(flags, BLOCK, axis=2)

    qt = all_q[:, rows:].reshape(groups_q * text_rows, width)
    kt = all_kv[0, :, rows:].reshape(groups_k * text_rows, width)
    vt = all_kv[1, :, rows:].reshape(groups_k * text_rows, width)

    numer, denom = attend(all_q, qt, all_kv, kt, vt, flags, heads, head_size)
    denom = denom[:, :, :heads]
    denom_hi = denom.astype(jnp.bfloat16)
    denom_lo = (denom - denom_hi.astype(jnp.float32)).astype(jnp.bfloat16)
    packed = jnp.concatenate([numer.astype(jnp.bfloat16), denom_hi, denom_lo], axis=2)
    sections = lax.axis_size("section")
    per = rows // sections
    lanes = packed.shape[2]
    image_rows = packed[:, :rows].reshape(groups_q, per, sections, lanes).transpose(2, 0, 1, 3)
    text_part = jnp.broadcast_to(packed[None, :, rows:], (sections, groups_q, text_rows, lanes))
    packed = jnp.concatenate([image_rows, text_part], axis=2)
    packed = packed.reshape(sections * groups_q, per + text_rows, lanes)
    packed = lax.all_to_all(packed, ("section", "qq"), split_axis=0, concat_axis=0, tiled=True)
    packed = packed.reshape(sections, groups_q, per + text_rows, lanes)
    packed = jnp.sum(packed.astype(jnp.float32), axis=1)
    numer = packed[:, :, :width].reshape(sections, per + text_rows, heads, head_size)
    denom = packed[:, :, width:width + heads] + packed[:, :, width + heads:]
    result = (numer / denom[..., None]).astype(jnp.bfloat16)
    image_out = result[:, :per].reshape(sections, per, width).transpose(1, 0, 2)
    image_out = image_out.reshape(per, 1, sections * width)
    own_section = lax.axis_index("section")
    text_out = lax.dynamic_index_in_dim(result[:, per:], own_section, axis=0, keepdims=False)
    text_out = text_out.reshape(text_rows, width)
    return (image_out, text_out)


def solution(mesh):
    sections, seq = mesh.devices.shape
    grid = Mesh(
        mesh.devices.reshape(sections, seq // QUERY_GROUP, QUERY_GROUP),
        ("section", "kk", "qq"),
    )
    rows = ("kk", "qq")
    placed = (
        P(rows, "section"),
        P(rows, "section"),
        P(rows, "section"),
        P(rows, "section"),
        P(rows, "section"),
        P(rows, "section"),
        P(),
        P("section", rows, None),
    )
    return jax.shard_map(
        body,
        mesh=grid,
        in_specs=placed,
        out_specs=(P(rows, "section", None), P(rows, "section")),
        check_vma=False,
    )
```

```python
import jax
import jax.numpy as jnp
from jax import lax
from jax.experimental import pallas as pl
from jax.experimental.pallas import tpu as pltpu
from jax.sharding import Mesh, PartitionSpec as P

BLOCK = 128
QUERY_GROUP = 4


def normed(values, gain, heads):
    rows = values.shape[0]
    floats = values.astype(jnp.float32).reshape(rows, heads, gain.shape[0])
    power = jnp.mean(floats * floats, axis=-1, keepdims=True)
    return (floats * lax.rsqrt(power + 1e-06) * gain).astype(jnp.bfloat16)


def attend_kernel(q_ref, qt_ref, ki_ref, kt_ref, vi_ref, vt_ref, fl_ref, num_ref, den_ref):
    head = pl.program_id(0)
    head_size = q_ref.shape[-1]
    scale = head_size ** (-0.5)
    q_blocks = q_ref.shape[0]
    text_rows = qt_ref.shape[0] // q_blocks
    dims = (((1,), (1,)), ((), ()))
    keys_img = ki_ref[0].reshape(-1, head_size)
    keys_txt = kt_ref[...]
    vals_img = vi_ref[0].reshape(-1, head_size)
    vals_txt = vt_ref[...]

    @pl.when(head == 0)
    def _():
        den_ref[...] = jnp.zeros(den_ref.shape, den_ref.dtype)

    def one(q, flags):
        s_img = lax.dot_general(q, keys_img, dims, preferred_element_type=jnp.float32) * scale
        s_txt = lax.dot_general(q, keys_txt, dims, preferred_element_type=jnp.float32) * scale
        e_img = jnp.exp(s_img)
        if flags is not None:
            e_img = jnp.where(flags > 0, e_img, jnp.float32(0.0))
        e_txt = jnp.exp(s_txt)
        den = jnp.sum(e_img, axis=1, keepdims=True) + jnp.sum(e_txt, axis=1, keepdims=True)
        num = jnp.dot(e_img.astype(jnp.bfloat16), vals_img, preferred_element_type=jnp.float32)
        num = num + jnp.dot(e_txt.astype(jnp.bfloat16), vals_txt, preferred_element_type=jnp.float32)
        return num, den

    def put(a, lo, hi, num, den):
        num_ref[a, lo:hi, :] = num
        lane = lax.broadcasted_iota(jnp.int32, (hi - lo, den_ref.shape[-1]), 1)
        den_ref[a, lo:hi, :] = jnp.where(lane == head, den, den_ref[a, lo:hi, :])

    for a in range(q_blocks):
        num, den = one(q_ref[a, 0:BLOCK, :], fl_ref[0, a:a + 1, :])
        put(a, 0, BLOCK, num, den)
    num, den = one(qt_ref[...], None)
    for a in range(q_blocks):
        part = slice(a * text_rows, (a + 1) * text_rows)
        put(a, BLOCK, BLOCK + text_rows, num[part], den[part])


def attend(all_q, qt, kv, kt, vt, fl, heads, head_size):
    groups_q, stride = all_q.shape[0], all_q.shape[1]
    groups_k = kv.shape[1]
    n_qt, n_kt = qt.shape[0], kt.shape[0]
    width = heads * head_size

    def cols(rows):
        return pl.BlockSpec((rows, head_size), lambda h: (0, h))

    return pl.pallas_call(
        attend_kernel,
        grid=(heads,),
        in_specs=[
            pl.BlockSpec((groups_q, stride, head_size), lambda h: (0, 0, h)),
            cols(n_qt),
            pl.BlockSpec((1, groups_k, BLOCK, head_size), lambda h: (0, 0, 0, h)),
            cols(n_kt),
            pl.BlockSpec((1, groups_k, BLOCK, head_size), lambda h: (1, 0, 0, h)),
            cols(n_kt),
            pl.BlockSpec((1,) + fl.shape[1:], lambda h: (h, 0, 0)),
        ],
        out_specs=[
            pl.BlockSpec((groups_q, stride, head_size), lambda h: (0, 0, h)),
            pl.BlockSpec((groups_q, stride, BLOCK), lambda h: (0, 0, 0)),
        ],
        out_shape=[
            jax.ShapeDtypeStruct((groups_q, stride, width), jnp.float32),
            jax.ShapeDtypeStruct((groups_q, stride, BLOCK), jnp.float32),
        ],
        compiler_params=pltpu.CompilerParams(vmem_limit_bytes=48 * 1024 * 1024),
    )(all_q, qt, kv, kt, kv, vt, fl)


def body(q_img, k_img, v_img, q_txt, k_txt, v_txt, norm_gains, block_map):
    rows, width = q_img.shape
    head_size = norm_gains.shape[1]
    heads = width // head_size
    text_rows = q_txt.shape[0]
    stride = rows + text_rows
    groups_q = lax.axis_size("qq")
    groups_k = lax.axis_size("kk")
    own_q = lax.axis_index("qq")

    queries = jnp.concatenate(
        [normed(q_img, norm_gains[0], heads), normed(q_txt, norm_gains[2], heads)], axis=0
    ).reshape(1, stride, width)
    keys = jnp.concatenate(
        [normed(k_img, norm_gains[1], heads), normed(k_txt, norm_gains[3], heads)], axis=0
    ).reshape(1, stride, width)
    values = jnp.concatenate([v_img, v_txt], axis=0).reshape(1, stride, width)
    pair = jnp.stack([keys, values], axis=0)

    all_q = lax.all_gather(queries, "qq", axis=0, tiled=True)
    all_kv = lax.all_gather(pair, "kk", axis=1, tiled=True)
    flags = lax.all_gather(block_map, "qq", axis=1, tiled=True)
    flags = flags.reshape(heads, groups_q, groups_k, groups_q)
    flags = lax.dynamic_index_in_dim(flags, own_q, axis=3, keepdims=False)
    flags = jnp.repeat(flags, BLOCK, axis=2)

    qt = all_q[:, rows:].reshape(groups_q * text_rows, width)
    kt = all_kv[0, :, rows:].reshape(groups_k * text_rows, width)
    vt = all_kv[1, :, rows:].reshape(groups_k * text_rows, width)

    numer, denom = attend(all_q, qt, all_kv, kt, vt, flags, heads, head_size)
    denom = denom[:, :, :heads]
    denom_hi = denom.astype(jnp.bfloat16)
    denom_lo = (denom - denom_hi.astype(jnp.float32)).astype(jnp.bfloat16)
    sections = lax.axis_size("section")
    per = rows // sections
    count = sections * groups_q

    def by_destination(part):
        lanes = part.shape[2]
        image_rows = part[:, :rows].reshape(groups_q, per, sections, lanes).transpose(2, 0, 1, 3)
        text_part = jnp.broadcast_to(part[None, :, rows:], (sections, groups_q, text_rows, lanes))
        part = jnp.concatenate([image_rows, text_part], axis=2)
        return part.reshape(count, -1)

    flat_num = by_destination(numer.astype(jnp.bfloat16))
    flat_den = by_destination(jnp.concatenate([denom_hi, denom_lo], axis=2))
    num_size, den_size = flat_num.shape[1], flat_den.shape[1]
    total = num_size + den_size
    padded = -(-total // (16 * BLOCK)) * (16 * BLOCK)
    packed = jnp.concatenate(
        [flat_num, flat_den, jnp.zeros((count, padded - total), jnp.bfloat16)], axis=1
    ).reshape(count, padded // BLOCK, BLOCK)
    packed = lax.all_to_all(packed, ("section", "qq"), split_axis=0, concat_axis=0, tiled=True)
    packed = packed.reshape(sections, groups_q, padded)
    numer = jnp.sum(packed[:, :, :num_size].astype(jnp.float32), axis=1)
    numer = numer.reshape(sections, per + text_rows, heads, head_size)
    denom = jnp.sum(packed[:, :, num_size:total].astype(jnp.float32), axis=1)
    denom = denom.reshape(sections, per + text_rows, 2, heads)
    denom = denom[:, :, 0] + denom[:, :, 1]
    result = (numer / denom[..., None]).astype(jnp.bfloat16)
    image_out = result[:, :per].reshape(sections, per, width).transpose(1, 0, 2)
    image_out = image_out.reshape(per, 1, sections * width)
    own_section = lax.axis_index("section")
    text_out = lax.dynamic_index_in_dim(result[:, per:], own_section, axis=0, keepdims=False)
    text_out = text_out.reshape(text_rows, width)
    return (image_out, text_out)


def solution(mesh):
    sections, seq = mesh.devices.shape
    grid = Mesh(
        mesh.devices.reshape(sections, seq // QUERY_GROUP, QUERY_GROUP),
        ("section", "kk", "qq"),
    )
    rows = ("kk", "qq")
    placed = (
        P(rows, "section"),
        P(rows, "section"),
        P(rows, "section"),
        P(rows, "section"),
        P(rows, "section"),
        P(rows, "section"),
        P(),
        P("section", rows, None),
    )
    return jax.shard_map(
        body,
        mesh=grid,
        in_specs=placed,
        out_specs=(P(rows, "section", None), P(rows, "section")),
        check_vma=False,
    )
```

```python
import math

import jax
import jax.numpy as jnp
from jax import lax
from jax.experimental import pallas as pl
from jax.experimental.pallas import tpu as pltpu
from jax.sharding import Mesh, PartitionSpec as P

BLOCK = 128
QUERY_GROUP = 4


def normed(values, gain, heads):
    rows = values.shape[0]
    floats = values.astype(jnp.float32).reshape(rows, heads, gain.shape[0])
    power = jnp.mean(floats * floats, axis=-1, keepdims=True)
    return (floats * lax.rsqrt(power + 1e-06) * gain).astype(jnp.bfloat16)


def attend_kernel(q_ref, qt_ref, ki_ref, kt_ref, vi_ref, vt_ref, fl_ref, num_ref, den_ref):
    head = pl.program_id(0)
    head_size = q_ref.shape[-1]
    scale = head_size ** (-0.5) * math.log2(math.e)
    q_blocks = q_ref.shape[0]
    text_rows = qt_ref.shape[0] // q_blocks
    dims = (((1,), (1,)), ((), ()))
    keys_img = ki_ref[0].reshape(-1, head_size)
    keys_txt = kt_ref[...]
    vals_img = vi_ref[0].reshape(-1, head_size)
    vals_txt = vt_ref[...]

    @pl.when(head == 0)
    def _():
        den_ref[...] = jnp.zeros(den_ref.shape, den_ref.dtype)

    def one(q, flags):
        s_img = lax.dot_general(q, keys_img, dims, preferred_element_type=jnp.float32) * scale
        s_txt = lax.dot_general(q, keys_txt, dims, preferred_element_type=jnp.float32) * scale
        e_img = jnp.exp2(s_img)
        if flags is not None:
            e_img = jnp.where(flags > 0, e_img, jnp.float32(0.0))
        e_txt = jnp.exp2(s_txt)
        den = jnp.sum(e_img, axis=1, keepdims=True) + jnp.sum(e_txt, axis=1, keepdims=True)
        num = jnp.dot(e_img.astype(jnp.bfloat16), vals_img, preferred_element_type=jnp.float32)
        num = num + jnp.dot(e_txt.astype(jnp.bfloat16), vals_txt, preferred_element_type=jnp.float32)
        return num, den

    def put(a, lo, hi, num, den):
        num_ref[a, lo:hi, :] = num
        lane = lax.broadcasted_iota(jnp.int32, (hi - lo, den_ref.shape[-1]), 1)
        den_ref[a, lo:hi, :] = jnp.where(lane == head, den, den_ref[a, lo:hi, :])

    for a in range(q_blocks):
        num, den = one(q_ref[a, 0:BLOCK, :], fl_ref[0, a:a + 1, :])
        put(a, 0, BLOCK, num, den)
    num, den = one(qt_ref[...], None)
    for a in range(q_blocks):
        part = slice(a * text_rows, (a + 1) * text_rows)
        put(a, BLOCK, BLOCK + text_rows, num[part], den[part])


def attend(all_q, qt, kv, kt, vt, fl, heads, head_size):
    groups_q, stride = all_q.shape[0], all_q.shape[1]
    groups_k = kv.shape[1]
    n_qt, n_kt = qt.shape[0], kt.shape[0]
    width = heads * head_size

    def cols(rows):
        return pl.BlockSpec((rows, head_size), lambda h: (0, h))

    return pl.pallas_call(
        attend_kernel,
        grid=(heads,),
        in_specs=[
            pl.BlockSpec((groups_q, stride, head_size), lambda h: (0, 0, h)),
            cols(n_qt),
            pl.BlockSpec((1, groups_k, BLOCK, head_size), lambda h: (0, 0, 0, h)),
            cols(n_kt),
            pl.BlockSpec((1, groups_k, BLOCK, head_size), lambda h: (1, 0, 0, h)),
            cols(n_kt),
            pl.BlockSpec((1,) + fl.shape[1:], lambda h: (h, 0, 0)),
        ],
        out_specs=[
            pl.BlockSpec((groups_q, stride, head_size), lambda h: (0, 0, h)),
            pl.BlockSpec((groups_q, stride, BLOCK), lambda h: (0, 0, 0)),
        ],
        out_shape=[
            jax.ShapeDtypeStruct((groups_q, stride, width), jnp.float32),
            jax.ShapeDtypeStruct((groups_q, stride, BLOCK), jnp.float32),
        ],
        compiler_params=pltpu.CompilerParams(vmem_limit_bytes=48 * 1024 * 1024),
    )(all_q, qt, kv, kt, kv, vt, fl)


def body(q_img, k_img, v_img, q_txt, k_txt, v_txt, norm_gains, block_map):
    rows, width = q_img.shape
    head_size = norm_gains.shape[1]
    heads = width // head_size
    text_rows = q_txt.shape[0]
    stride = rows + text_rows
    groups_q = lax.axis_size("qq")
    groups_k = lax.axis_size("kk")
    own_q = lax.axis_index("qq")

    queries = jnp.concatenate(
        [normed(q_img, norm_gains[0], heads), normed(q_txt, norm_gains[2], heads)], axis=0
    ).reshape(1, stride, width)
    keys = jnp.concatenate(
        [normed(k_img, norm_gains[1], heads), normed(k_txt, norm_gains[3], heads)], axis=0
    ).reshape(1, stride, width)
    values = jnp.concatenate([v_img, v_txt], axis=0).reshape(1, stride, width)
    pair = jnp.stack([keys, values], axis=0)

    all_q = lax.all_gather(queries, "qq", axis=0, tiled=True)
    all_kv = lax.all_gather(pair, "kk", axis=1, tiled=True)
    flags = lax.all_gather(block_map, "qq", axis=1, tiled=True)
    flags = flags.reshape(heads, groups_q, groups_k, groups_q)
    flags = lax.dynamic_index_in_dim(flags, own_q, axis=3, keepdims=False)
    flags = jnp.repeat(flags, BLOCK, axis=2)

    qt = all_q[:, rows:].reshape(groups_q * text_rows, width)
    kt = all_kv[0, :, rows:].reshape(groups_k * text_rows, width)
    vt = all_kv[1, :, rows:].reshape(groups_k * text_rows, width)

    numer, denom = attend(all_q, qt, all_kv, kt, vt, flags, heads, head_size)
    denom = denom[:, :, :heads]
    denom_hi = denom.astype(jnp.bfloat16)
    denom_lo = (denom - denom_hi.astype(jnp.float32)).astype(jnp.bfloat16)
    sections = lax.axis_size("section")
    per = rows // sections
    count = sections * groups_q

    def by_destination(part):
        lanes = part.shape[2]
        image_rows = part[:, :rows].reshape(groups_q, per, sections, lanes).transpose(2, 0, 1, 3)
        text_part = jnp.broadcast_to(part[None, :, rows:], (sections, groups_q, text_rows, lanes))
        part = jnp.concatenate([image_rows, text_part], axis=2)
        return part.reshape(count, -1)

    flat_num = by_destination(numer.astype(jnp.bfloat16))
    flat_den = by_destination(jnp.concatenate([denom_hi, denom_lo], axis=2))
    num_size, den_size = flat_num.shape[1], flat_den.shape[1]
    total = num_size + den_size
    padded = -(-total // (16 * BLOCK)) * (16 * BLOCK)
    packed = jnp.concatenate(
        [flat_num, flat_den, jnp.zeros((count, padded - total), jnp.bfloat16)], axis=1
    ).reshape(count, padded // BLOCK, BLOCK)
    packed = lax.all_to_all(packed, ("section", "qq"), split_axis=0, concat_axis=0, tiled=True)
    packed = packed.reshape(sections, groups_q, padded)
    numer = jnp.sum(packed[:, :, :num_size].astype(jnp.float32), axis=1)
    numer = numer.reshape(sections, per + text_rows, heads, head_size)
    denom = jnp.sum(packed[:, :, num_size:total].astype(jnp.float32), axis=1)
    denom = denom.reshape(sections, per + text_rows, 2, heads)
    denom = denom[:, :, 0] + denom[:, :, 1]
    result = (numer / denom[..., None]).astype(jnp.bfloat16)
    image_out = result[:, :per].reshape(sections, per, width).transpose(1, 0, 2)
    image_out = image_out.reshape(per, 1, sections * width)
    own_section = lax.axis_index("section")
    text_out = lax.dynamic_index_in_dim(result[:, per:], own_section, axis=0, keepdims=False)
    text_out = text_out.reshape(text_rows, width)
    return (image_out, text_out)


def solution(mesh):
    sections, seq = mesh.devices.shape
    grid = Mesh(
        mesh.devices.reshape(sections, seq // QUERY_GROUP, QUERY_GROUP),
        ("section", "kk", "qq"),
    )
    rows = ("kk", "qq")
    placed = (
        P(rows, "section"),
        P(rows, "section"),
        P(rows, "section"),
        P(rows, "section"),
        P(rows, "section"),
        P(rows, "section"),
        P(),
        P("section", rows, None),
    )
    return jax.shard_map(
        body,
        mesh=grid,
        in_specs=placed,
        out_specs=(P(rows, "section", None), P(rows, "section")),
        check_vma=False,
    )
```

```python
import jax
import jax.numpy as jnp
from jax import lax
from jax.experimental import pallas as pl
from jax.experimental.pallas import tpu as pltpu
from jax.sharding import Mesh, PartitionSpec as P

BLOCK = 128
QUERY_GROUP = 4


def normed(values, gain, heads):
    rows = values.shape[0]
    floats = values.astype(jnp.float32).reshape(rows, heads, gain.shape[0])
    power = jnp.mean(floats * floats, axis=-1, keepdims=True)
    return (floats * lax.rsqrt(power + 1e-06) * gain).astype(jnp.bfloat16)


def attend_kernel(q_ref, qt_ref, ki_ref, kt_ref, vi_ref, vt_ref, fl_ref, num_ref, den_ref):
    head = pl.program_id(0)
    head_size = q_ref.shape[-1]
    scale = head_size ** (-0.5)
    q_blocks = q_ref.shape[0]
    text_rows = qt_ref.shape[0] // q_blocks
    dims = (((1,), (1,)), ((), ()))
    keys_img = ki_ref[...].reshape(-1, head_size)
    keys_txt = kt_ref[...]
    vals_img = vi_ref[...].reshape(-1, head_size)
    vals_txt = vt_ref[...]

    @pl.when(head == 0)
    def _():
        den_ref[...] = jnp.zeros(den_ref.shape, den_ref.dtype)

    def one(q, flags):
        s_img = lax.dot_general(q, keys_img, dims, preferred_element_type=jnp.float32) * scale
        s_txt = lax.dot_general(q, keys_txt, dims, preferred_element_type=jnp.float32) * scale
        e_img = jnp.exp(s_img)
        if flags is not None:
            e_img = jnp.where(flags > 0, e_img, jnp.float32(0.0))
        e_txt = jnp.exp(s_txt)
        den = jnp.sum(e_img, axis=1, keepdims=True) + jnp.sum(e_txt, axis=1, keepdims=True)
        num = jnp.dot(e_img.astype(jnp.bfloat16), vals_img, preferred_element_type=jnp.float32)
        num = num + jnp.dot(e_txt.astype(jnp.bfloat16), vals_txt, preferred_element_type=jnp.float32)
        return num, den

    def put(a, lo, hi, num, den):
        num_ref[a, lo:hi, :] = num
        lane = lax.broadcasted_iota(jnp.int32, (hi - lo, den_ref.shape[-1]), 1)
        den_ref[a, lo:hi, :] = jnp.where(lane == head, den, den_ref[a, lo:hi, :])

    for a in range(q_blocks):
        num, den = one(q_ref[a, 0:BLOCK, :], fl_ref[0, a:a + 1, :])
        put(a, 0, BLOCK, num, den)
    num, den = one(qt_ref[...], None)
    for a in range(q_blocks):
        part = slice(a * text_rows, (a + 1) * text_rows)
        put(a, BLOCK, BLOCK + text_rows, num[part], den[part])


def attend(all_q, qt, kv, kt, vt, fl, heads, head_size):
    groups_q, stride = all_q.shape[0], all_q.shape[1]
    groups_k = kv.shape[0]
    n_qt, n_kt = qt.shape[0], kt.shape[0]
    width = heads * head_size

    def cols(rows):
        return pl.BlockSpec((rows, head_size), lambda h: (0, h))

    return pl.pallas_call(
        attend_kernel,
        grid=(heads,),
        in_specs=[
            pl.BlockSpec((groups_q, stride, head_size), lambda h: (0, 0, h)),
            cols(n_qt),
            pl.BlockSpec((groups_k, BLOCK, head_size), lambda h: (0, 0, h)),
            cols(n_kt),
            pl.BlockSpec((groups_k, BLOCK, head_size), lambda h: (0, 1, h)),
            cols(n_kt),
            pl.BlockSpec((1,) + fl.shape[1:], lambda h: (h, 0, 0)),
        ],
        out_specs=[
            pl.BlockSpec((groups_q, stride, head_size), lambda h: (0, 0, h)),
            pl.BlockSpec((groups_q, stride, BLOCK), lambda h: (0, 0, 0)),
        ],
        out_shape=[
            jax.ShapeDtypeStruct((groups_q, stride, width), jnp.float32),
            jax.ShapeDtypeStruct((groups_q, stride, BLOCK), jnp.float32),
        ],
        compiler_params=pltpu.CompilerParams(vmem_limit_bytes=48 * 1024 * 1024),
    )(all_q, qt, kv, kt, kv, vt, fl)


def body(q_img, k_img, v_img, q_txt, k_txt, v_txt, norm_gains, block_map):
    rows, width = q_img.shape
    head_size = norm_gains.shape[1]
    heads = width // head_size
    text_rows = q_txt.shape[0]
    stride = rows + text_rows
    groups_q = lax.axis_size("qq")
    groups_k = lax.axis_size("kk")
    own_q = lax.axis_index("qq")

    queries = jnp.concatenate(
        [normed(q_img, norm_gains[0], heads), normed(q_txt, norm_gains[2], heads)], axis=0
    ).reshape(1, stride, width)
    keys_image = normed(k_img, norm_gains[1], heads).reshape(rows, width)
    keys_text = normed(k_txt, norm_gains[3], heads).reshape(text_rows, width)
    pair = jnp.concatenate([keys_image, v_img, keys_text, v_txt], axis=0)[None]

    all_q = lax.all_gather(queries, "qq", axis=0, tiled=True)
    all_kv = lax.all_gather(pair, "kk", axis=0, tiled=True)
    flags = lax.all_gather(block_map, "qq", axis=1, tiled=True)
    flags = flags.reshape(heads, groups_q, groups_k, groups_q)
    flags = lax.dynamic_index_in_dim(flags, own_q, axis=3, keepdims=False)
    flags = jnp.repeat(flags, BLOCK, axis=2)

    qt = all_q[:, rows:].reshape(groups_q * text_rows, width)
    kt = all_kv[:, 2 * rows:2 * rows + text_rows].reshape(groups_k * text_rows, width)
    vt = all_kv[:, 2 * rows + text_rows:].reshape(groups_k * text_rows, width)

    numer, denom = attend(all_q, qt, all_kv, kt, vt, flags, heads, head_size)
    denom = denom[:, :, :heads]
    denom_hi = denom.astype(jnp.bfloat16)
    denom_lo = (denom - denom_hi.astype(jnp.float32)).astype(jnp.bfloat16)
    sections = lax.axis_size("section")
    per = rows // sections
    count = sections * groups_q

    def by_destination(part):
        lanes = part.shape[2]
        image_rows = part[:, :rows].reshape(groups_q, per, sections, lanes).transpose(2, 0, 1, 3)
        text_part = jnp.broadcast_to(part[None, :, rows:], (sections, groups_q, text_rows, lanes))
        part = jnp.concatenate([image_rows, text_part], axis=2)
        return part.reshape(count, -1)

    flat_num = by_destination(numer.astype(jnp.bfloat16))
    flat_den = by_destination(jnp.concatenate([denom_hi, denom_lo], axis=2))
    num_size, den_size = flat_num.shape[1], flat_den.shape[1]
    total = num_size + den_size
    padded = -(-total // (16 * BLOCK)) * (16 * BLOCK)
    packed = jnp.concatenate(
        [flat_num, flat_den, jnp.zeros((count, padded - total), jnp.bfloat16)], axis=1
    ).reshape(count, padded // BLOCK, BLOCK)
    packed = lax.all_to_all(packed, ("section", "qq"), split_axis=0, concat_axis=0, tiled=True)
    packed = packed.reshape(sections, groups_q, padded)
    numer = jnp.sum(packed[:, :, :num_size].astype(jnp.float32), axis=1)
    numer = numer.reshape(sections, per + text_rows, heads, head_size)
    denom = jnp.sum(packed[:, :, num_size:total].astype(jnp.float32), axis=1)
    denom = denom.reshape(sections, per + text_rows, 2, heads)
    denom = denom[:, :, 0] + denom[:, :, 1]
    result = (numer / denom[..., None]).astype(jnp.bfloat16)
    image_out = result[:, :per].reshape(sections, per, width).transpose(1, 0, 2)
    image_out = image_out.reshape(per, 1, sections * width)
    own_section = lax.axis_index("section")
    text_out = lax.dynamic_index_in_dim(result[:, per:], own_section, axis=0, keepdims=False)
    text_out = text_out.reshape(text_rows, width)
    return (image_out, text_out)


def solution(mesh):
    sections, seq = mesh.devices.shape
    grid = Mesh(
        mesh.devices.reshape(sections, seq // QUERY_GROUP, QUERY_GROUP),
        ("section", "kk", "qq"),
    )
    rows = ("kk", "qq")
    placed = (
        P(rows, "section"),
        P(rows, "section"),
        P(rows, "section"),
        P(rows, "section"),
        P(rows, "section"),
        P(rows, "section"),
        P(),
        P("section", rows, None),
    )
    return jax.shard_map(
        body,
        mesh=grid,
        in_specs=placed,
        out_specs=(P(rows, "section", None), P(rows, "section")),
        check_vma=False,
    )
```

```python
import jax
import jax.numpy as jnp
from jax import lax
from jax.experimental import pallas as pl
from jax.experimental.pallas import tpu as pltpu
from jax.sharding import Mesh, PartitionSpec as P

BLOCK = 128
QUERY_GROUP = 4


def normed(values, gain, heads):
    rows = values.shape[0]
    floats = values.astype(jnp.float32).reshape(rows, heads, gain.shape[0])
    power = jnp.mean(floats * floats, axis=-1, keepdims=True)
    return (floats * lax.rsqrt(power + 1e-06) * gain).astype(jnp.bfloat16)


def attend_kernel(q_ref, qt_ref, ki_ref, kt_ref, vi_ref, vt_ref, fl_ref, num_ref, den_ref):
    head = pl.program_id(0)
    head_size = q_ref.shape[-1]
    scale = head_size ** (-0.5)
    q_blocks = q_ref.shape[0]
    text_rows = qt_ref.shape[0] // q_blocks
    dims = (((1,), (1,)), ((), ()))
    keys_img = ki_ref[0].reshape(-1, head_size)
    keys_txt = kt_ref[...]
    vals_img = vi_ref[0].reshape(-1, head_size)
    vals_txt = vt_ref[...]

    @pl.when(head == 0)
    def _():
        den_ref[...] = jnp.zeros(den_ref.shape, den_ref.dtype)

    def one(q, flags):
        s_img = lax.dot_general(q, keys_img, dims, preferred_element_type=jnp.float32) * scale
        s_txt = lax.dot_general(q, keys_txt, dims, preferred_element_type=jnp.float32) * scale
        e_img = jnp.exp(s_img)
        if flags is not None:
            e_img = jnp.where(flags > 0, e_img, jnp.float32(0.0))
        e_txt = jnp.exp(s_txt)
        den = jnp.sum(e_img, axis=1, keepdims=True) + jnp.sum(e_txt, axis=1, keepdims=True)
        num = jnp.dot(e_img.astype(jnp.bfloat16), vals_img, preferred_element_type=jnp.float32)
        num = num + jnp.dot(e_txt.astype(jnp.bfloat16), vals_txt, preferred_element_type=jnp.float32)
        return num, den

    def put(a, lo, hi, num, den):
        num_ref[a, lo:hi, :] = num
        lane = lax.broadcasted_iota(jnp.int32, (hi - lo, den_ref.shape[-1]), 1)
        den_ref[a, lo:hi, :] = jnp.where(lane == head, den, den_ref[a, lo:hi, :])

    for a in range(q_blocks):
        num, den = one(q_ref[a, 0:BLOCK, :], fl_ref[0, a:a + 1, :])
        put(a, 0, BLOCK, num, den)
    num, den = one(qt_ref[...], None)
    for a in range(q_blocks):
        part = slice(a * text_rows, (a + 1) * text_rows)
        put(a, BLOCK, BLOCK + text_rows, num[part], den[part])


def attend(all_q, qt, kv, kt, vt, fl, heads, head_size):
    groups_q, stride = all_q.shape[0], all_q.shape[1]
    groups_k = kv.shape[1]
    n_qt, n_kt = qt.shape[0], kt.shape[0]
    width = heads * head_size

    def cols(rows):
        return pl.BlockSpec((rows, head_size), lambda h: (0, h))

    return pl.pallas_call(
        attend_kernel,
        grid=(heads,),
        in_specs=[
            pl.BlockSpec((groups_q, stride, head_size), lambda h: (0, 0, h)),
            cols(n_qt),
            pl.BlockSpec((1, groups_k, BLOCK, head_size), lambda h: (0, 0, 0, h)),
            cols(n_kt),
            pl.BlockSpec((1, groups_k, BLOCK, head_size), lambda h: (1, 0, 0, h)),
            cols(n_kt),
            pl.BlockSpec((1,) + fl.shape[1:], lambda h: (h, 0, 0)),
        ],
        out_specs=[
            pl.BlockSpec((groups_q, stride, head_size), lambda h: (0, 0, h)),
            pl.BlockSpec((groups_q, stride, BLOCK), lambda h: (0, 0, 0)),
        ],
        out_shape=[
            jax.ShapeDtypeStruct((groups_q, stride, width), jnp.float32),
            jax.ShapeDtypeStruct((groups_q, stride, BLOCK), jnp.float32),
        ],
        compiler_params=pltpu.CompilerParams(vmem_limit_bytes=48 * 1024 * 1024),
    )(all_q, qt, kv, kt, kv, vt, fl)


def body(q_img, k_img, v_img, q_txt, k_txt, v_txt, norm_gains, block_map):
    rows, width = q_img.shape
    head_size = norm_gains.shape[1]
    heads = width // head_size
    text_rows = q_txt.shape[0]
    stride = rows + text_rows
    groups_q = lax.axis_size("qq")
    groups_k = lax.axis_size("kk")
    own_q = lax.axis_index("qq")

    queries = jnp.concatenate(
        [normed(q_img, norm_gains[0], heads), normed(q_txt, norm_gains[2], heads)], axis=0
    ).reshape(1, stride, width)
    keys = jnp.concatenate(
        [normed(k_img, norm_gains[1], heads), normed(k_txt, norm_gains[3], heads)], axis=0
    ).reshape(1, stride, width)
    values = jnp.concatenate([v_img, v_txt], axis=0).reshape(1, stride, width)
    pair = jnp.stack([keys, values], axis=0)

    all_q = lax.all_gather(queries, "qq", axis=0, tiled=True)
    spread = jnp.broadcast_to(pair, (2, groups_k) + pair.shape[2:])
    all_kv = lax.all_to_all(spread, "kk", split_axis=1, concat_axis=1, tiled=True)
    flags = lax.all_gather(block_map, "qq", axis=1, tiled=True)
    flags = flags.reshape(heads, groups_q, groups_k, groups_q)
    flags = lax.dynamic_index_in_dim(flags, own_q, axis=3, keepdims=False)
    flags = jnp.repeat(flags, BLOCK, axis=2)

    qt = all_q[:, rows:].reshape(groups_q * text_rows, width)
    kt = all_kv[0, :, rows:].reshape(groups_k * text_rows, width)
    vt = all_kv[1, :, rows:].reshape(groups_k * text_rows, width)

    numer, denom = attend(all_q, qt, all_kv, kt, vt, flags, heads, head_size)
    denom = denom[:, :, :heads]
    denom_hi = denom.astype(jnp.bfloat16)
    denom_lo = (denom - denom_hi.astype(jnp.float32)).astype(jnp.bfloat16)
    sections = lax.axis_size("section")
    per = rows // sections
    count = sections * groups_q

    def by_destination(part):
        lanes = part.shape[2]
        image_rows = part[:, :rows].reshape(groups_q, per, sections, lanes).transpose(2, 0, 1, 3)
        text_part = jnp.broadcast_to(part[None, :, rows:], (sections, groups_q, text_rows, lanes))
        part = jnp.concatenate([image_rows, text_part], axis=2)
        return part.reshape(count, -1)

    flat_num = by_destination(numer.astype(jnp.bfloat16))
    flat_den = by_destination(jnp.concatenate([denom_hi, denom_lo], axis=2))
    num_size, den_size = flat_num.shape[1], flat_den.shape[1]
    total = num_size + den_size
    padded = -(-total // (16 * BLOCK)) * (16 * BLOCK)
    packed = jnp.concatenate(
        [flat_num, flat_den, jnp.zeros((count, padded - total), jnp.bfloat16)], axis=1
    ).reshape(count, padded // BLOCK, BLOCK)
    packed = lax.all_to_all(packed, ("section", "qq"), split_axis=0, concat_axis=0, tiled=True)
    packed = packed.reshape(sections, groups_q, padded)
    numer = jnp.sum(packed[:, :, :num_size].astype(jnp.float32), axis=1)
    numer = numer.reshape(sections, per + text_rows, heads, head_size)
    denom = jnp.sum(packed[:, :, num_size:total].astype(jnp.float32), axis=1)
    denom = denom.reshape(sections, per + text_rows, 2, heads)
    denom = denom[:, :, 0] + denom[:, :, 1]
    result = (numer / denom[..., None]).astype(jnp.bfloat16)
    image_out = result[:, :per].reshape(sections, per, width).transpose(1, 0, 2)
    image_out = image_out.reshape(per, 1, sections * width)
    own_section = lax.axis_index("section")
    text_out = lax.dynamic_index_in_dim(result[:, per:], own_section, axis=0, keepdims=False)
    text_out = text_out.reshape(text_rows, width)
    return (image_out, text_out)


def solution(mesh):
    sections, seq = mesh.devices.shape
    grid = Mesh(
        mesh.devices.reshape(sections, seq // QUERY_GROUP, QUERY_GROUP),
        ("section", "kk", "qq"),
    )
    rows = ("kk", "qq")
    placed = (
        P(rows, "section"),
        P(rows, "section"),
        P(rows, "section"),
        P(rows, "section"),
        P(rows, "section"),
        P(rows, "section"),
        P(),
        P("section", rows, None),
    )
    return jax.shard_map(
        body,
        mesh=grid,
        in_specs=placed,
        out_specs=(P(rows, "section", None), P(rows, "section")),
        check_vma=False,
    )
```

```python
import jax
import jax.numpy as jnp
from jax import lax
from jax.experimental import pallas as pl
from jax.experimental.pallas import tpu as pltpu
from jax.sharding import Mesh, PartitionSpec as P

BLOCK = 128
QUERY_GROUP = 4


def normed(values, gain, heads):
    rows = values.shape[0]
    floats = values.astype(jnp.float32).reshape(rows, heads, gain.shape[0])
    power = jnp.mean(floats * floats, axis=-1, keepdims=True)
    return (floats * lax.rsqrt(power + 1e-06) * gain).astype(jnp.bfloat16)


def attend_kernel(fl_ref, q_ref, qt_ref, ki_ref, kt_ref, vi_ref, vt_ref, num_ref, den_ref):
    head = pl.program_id(0)
    head_size = q_ref.shape[-1]
    scale = head_size ** (-0.5)
    q_blocks = q_ref.shape[0]
    k_blocks = ki_ref.shape[1]
    text_rows = qt_ref.shape[0] // q_blocks
    dims = (((1,), (1,)), ((), ()))
    keys_txt = kt_ref[...]
    vals_txt = vt_ref[...]

    @pl.when(head == 0)
    def _():
        den_ref[...] = jnp.zeros(den_ref.shape, den_ref.dtype)

    def weigh(q, keys):
        s = lax.dot_general(q, keys, dims, preferred_element_type=jnp.float32) * scale
        return jnp.exp(s)

    def put(a, lo, hi, num, den):
        num_ref[a, lo:hi, :] = num
        lane = lax.broadcasted_iota(jnp.int32, (hi - lo, den_ref.shape[-1]), 1)
        den_ref[a, lo:hi, :] = jnp.where(lane == head, den, den_ref[a, lo:hi, :])

    for a in range(q_blocks):
        q = q_ref[a, 0:BLOCK, :]
        e_txt = weigh(q, keys_txt)
        start = (
            jnp.dot(e_txt.astype(jnp.bfloat16), vals_txt, preferred_element_type=jnp.float32),
            jnp.sum(e_txt, axis=1, keepdims=True),
        )

        def step(b, carry):
            def take(carry):
                num, den = carry
                e = weigh(q, ki_ref[0, b])
                num = num + jnp.dot(e.astype(jnp.bfloat16), vi_ref[0, b], preferred_element_type=jnp.float32)
                return num, den + jnp.sum(e, axis=1, keepdims=True)

            flag = fl_ref[(head * q_blocks + a) * k_blocks + b]
            return lax.cond(flag > 0, take, lambda c: c, carry)

        num, den = lax.fori_loop(0, k_blocks, step, start)
        put(a, 0, BLOCK, num, den)

    keys_img = ki_ref[0].reshape(-1, head_size)
    vals_img = vi_ref[0].reshape(-1, head_size)
    qt = qt_ref[...]
    e_img = weigh(qt, keys_img)
    e_txt = weigh(qt, keys_txt)
    den = jnp.sum(e_img, axis=1, keepdims=True) + jnp.sum(e_txt, axis=1, keepdims=True)
    num = jnp.dot(e_img.astype(jnp.bfloat16), vals_img, preferred_element_type=jnp.float32)
    num = num + jnp.dot(e_txt.astype(jnp.bfloat16), vals_txt, preferred_element_type=jnp.float32)
    for a in range(q_blocks):
        part = slice(a * text_rows, (a + 1) * text_rows)
        put(a, BLOCK, BLOCK + text_rows, num[part], den[part])


def attend(all_q, qt, kv, kt, vt, fl, heads, head_size):
    groups_q, stride = all_q.shape[0], all_q.shape[1]
    groups_k = kv.shape[1]
    n_qt, n_kt = qt.shape[0], kt.shape[0]
    width = heads * head_size

    def cols(rows):
        return pl.BlockSpec((rows, head_size), lambda h, f: (0, h))

    grid_spec = pltpu.PrefetchScalarGridSpec(
        num_scalar_prefetch=1,
        grid=(heads,),
        in_specs=[
            pl.BlockSpec((groups_q, stride, head_size), lambda h, f: (0, 0, h)),
            cols(n_qt),
            pl.BlockSpec((1, groups_k, BLOCK, head_size), lambda h, f: (0, 0, 0, h)),
            cols(n_kt),
            pl.BlockSpec((1, groups_k, BLOCK, head_size), lambda h, f: (1, 0, 0, h)),
            cols(n_kt),
        ],
        out_specs=[
            pl.BlockSpec((groups_q, stride, head_size), lambda h, f: (0, 0, h)),
            pl.BlockSpec((groups_q, stride, BLOCK), lambda h, f: (0, 0, 0)),
        ],
    )
    return pl.pallas_call(
        attend_kernel,
        grid_spec=grid_spec,
        out_shape=[
            jax.ShapeDtypeStruct((groups_q, stride, width), jnp.float32),
            jax.ShapeDtypeStruct((groups_q, stride, BLOCK), jnp.float32),
        ],
        compiler_params=pltpu.CompilerParams(vmem_limit_bytes=48 * 1024 * 1024),
    )(fl.reshape(-1), all_q, qt, kv, kt, kv, vt)


def body(q_img, k_img, v_img, q_txt, k_txt, v_txt, norm_gains, block_map):
    rows, width = q_img.shape
    head_size = norm_gains.shape[1]
    heads = width // head_size
    text_rows = q_txt.shape[0]
    stride = rows + text_rows
    groups_q = lax.axis_size("qq")
    groups_k = lax.axis_size("kk")
    own_q = lax.axis_index("qq")

    queries = jnp.concatenate(
        [normed(q_img, norm_gains[0], heads), normed(q_txt, norm_gains[2], heads)], axis=0
    ).reshape(1, stride, width)
    keys = jnp.concatenate(
        [normed(k_img, norm_gains[1], heads), normed(k_txt, norm_gains[3], heads)], axis=0
    ).reshape(1, stride, width)
    values = jnp.concatenate([v_img, v_txt], axis=0).reshape(1, stride, width)
    pair = jnp.stack([keys, values], axis=0)

    all_q = lax.all_gather(queries, "qq", axis=0, tiled=True)
    all_kv = lax.all_gather(pair, "kk", axis=1, tiled=True)
    flags = lax.all_gather(block_map, "qq", axis=1, tiled=True)
    flags = flags.reshape(heads, groups_q, groups_k, groups_q)
    flags = lax.dynamic_index_in_dim(flags, own_q, axis=3, keepdims=False)
    flags = (flags > 0).astype(jnp.int32)

    qt = all_q[:, rows:].reshape(groups_q * text_rows, width)
    kt = all_kv[0, :, rows:].reshape(groups_k * text_rows, width)
    vt = all_kv[1, :, rows:].reshape(groups_k * text_rows, width)

    numer, denom = attend(all_q, qt, all_kv, kt, vt, flags, heads, head_size)
    denom = denom[:, :, :heads]
    denom_hi = denom.astype(jnp.bfloat16)
    denom_lo = (denom - denom_hi.astype(jnp.float32)).astype(jnp.bfloat16)
    sections = lax.axis_size("section")
    per = rows // sections
    count = sections * groups_q

    def by_destination(part):
        lanes = part.shape[2]
        image_rows = part[:, :rows].reshape(groups_q, per, sections, lanes).transpose(2, 0, 1, 3)
        text_part = jnp.broadcast_to(part[None, :, rows:], (sections, groups_q, text_rows, lanes))
        part = jnp.concatenate([image_rows, text_part], axis=2)
        return part.reshape(count, -1)

    flat_num = by_destination(numer.astype(jnp.bfloat16))
    flat_den = by_destination(jnp.concatenate([denom_hi, denom_lo], axis=2))
    num_size, den_size = flat_num.shape[1], flat_den.shape[1]
    total = num_size + den_size
    padded = -(-total // (16 * BLOCK)) * (16 * BLOCK)
    packed = jnp.concatenate(
        [flat_num, flat_den, jnp.zeros((count, padded - total), jnp.bfloat16)], axis=1
    ).reshape(count, padded // BLOCK, BLOCK)
    packed = lax.all_to_all(packed, ("section", "qq"), split_axis=0, concat_axis=0, tiled=True)
    packed = packed.reshape(sections, groups_q, padded)
    numer = jnp.sum(packed[:, :, :num_size].astype(jnp.float32), axis=1)
    numer = numer.reshape(sections, per + text_rows, heads, head_size)
    denom = jnp.sum(packed[:, :, num_size:total].astype(jnp.float32), axis=1)
    denom = denom.reshape(sections, per + text_rows, 2, heads)
    denom = denom[:, :, 0] + denom[:, :, 1]
    result = (numer / denom[..., None]).astype(jnp.bfloat16)
    image_out = result[:, :per].reshape(sections, per, width).transpose(1, 0, 2)
    image_out = image_out.reshape(per, 1, sections * width)
    own_section = lax.axis_index("section")
    text_out = lax.dynamic_index_in_dim(result[:, per:], own_section, axis=0, keepdims=False)
    text_out = text_out.reshape(text_rows, width)
    return (image_out, text_out)


def solution(mesh):
    sections, seq = mesh.devices.shape
    grid = Mesh(
        mesh.devices.reshape(sections, seq // QUERY_GROUP, QUERY_GROUP),
        ("section", "kk", "qq"),
    )
    rows = ("kk", "qq")
    placed = (
        P(rows, "section"),
        P(rows, "section"),
        P(rows, "section"),
        P(rows, "section"),
        P(rows, "section"),
        P(rows, "section"),
        P(),
        P("section", rows, None),
    )
    return jax.shard_map(
        body,
        mesh=grid,
        in_specs=placed,
        out_specs=(P(rows, "section", None), P(rows, "section")),
        check_vma=False,
    )
```

```python
import jax
import jax.numpy as jnp
from jax import lax
from jax.experimental import pallas as pl
from jax.experimental.pallas import tpu as pltpu
from jax.sharding import Mesh, PartitionSpec as P

BLOCK = 128
QUERY_GROUP = 4


def normed(values, gain, heads):
    rows = values.shape[0]
    floats = values.astype(jnp.float32).reshape(rows, heads, gain.shape[0])
    power = jnp.mean(floats * floats, axis=-1, keepdims=True)
    return (floats * lax.rsqrt(power + 1e-06) * gain).astype(jnp.bfloat16)


def attend_kernel(q_ref, qt_ref, ki_ref, kt_ref, vi_ref, vt_ref, fl_ref, num_ref, den_ref):
    head = pl.program_id(0)
    head_size = q_ref.shape[-1]
    scale = head_size ** (-0.5)
    q_blocks = q_ref.shape[0]
    text_rows = qt_ref.shape[0] // q_blocks
    dims = (((1,), (1,)), ((), ()))
    keys_img = ki_ref[0].reshape(-1, head_size)
    keys_txt = kt_ref[...]
    vals_img = vi_ref[0].reshape(-1, head_size)
    vals_txt = vt_ref[...]

    @pl.when(head == 0)
    def _():
        den_ref[...] = jnp.zeros(den_ref.shape, den_ref.dtype)

    def one(q, flags):
        s_img = lax.dot_general(q, keys_img, dims, preferred_element_type=jnp.float32) * scale
        s_txt = lax.dot_general(q, keys_txt, dims, preferred_element_type=jnp.float32) * scale
        e_img = jnp.exp(s_img)
        if flags is not None:
            e_img = jnp.where(flags > 0, e_img, jnp.float32(0.0))
        e_txt = jnp.exp(s_txt)
        den = jnp.sum(e_img, axis=1, keepdims=True) + jnp.sum(e_txt, axis=1, keepdims=True)
        num = jnp.dot(e_img.astype(jnp.bfloat16), vals_img, preferred_element_type=jnp.float32)
        num = num + jnp.dot(e_txt.astype(jnp.bfloat16), vals_txt, preferred_element_type=jnp.float32)
        return num, den

    def put(a, lo, hi, num, den):
        num_ref[a, lo:hi, :] = num
        lane = lax.broadcasted_iota(jnp.int32, (hi - lo, den_ref.shape[-1]), 1)
        den_ref[a, lo:hi, :] = jnp.where(lane == head, den, den_ref[a, lo:hi, :])

    for a in range(q_blocks):
        num, den = one(q_ref[a, 0:BLOCK, :], fl_ref[0, a:a + 1, :])
        put(a, 0, BLOCK, num, den)
    num, den = one(qt_ref[...], None)
    for a in range(q_blocks):
        part = slice(a * text_rows, (a + 1) * text_rows)
        put(a, BLOCK, BLOCK + text_rows, num[part], den[part])


def attend(all_q, qt, kv, kt, vt, fl, heads, head_size):
    groups_q, stride = all_q.shape[0], all_q.shape[1]
    groups_k = kv.shape[1]
    n_qt, n_kt = qt.shape[0], kt.shape[0]
    width = heads * head_size

    def cols(rows):
        return pl.BlockSpec((rows, head_size), lambda h: (0, h))

    return pl.pallas_call(
        attend_kernel,
        grid=(heads,),
        in_specs=[
            pl.BlockSpec((groups_q, stride, head_size), lambda h: (0, 0, h)),
            cols(n_qt),
            pl.BlockSpec((1, groups_k, BLOCK, head_size), lambda h: (0, 0, 0, h)),
            cols(n_kt),
            pl.BlockSpec((1, groups_k, BLOCK, head_size), lambda h: (1, 0, 0, h)),
            cols(n_kt),
            pl.BlockSpec((1,) + fl.shape[1:], lambda h: (h, 0, 0)),
        ],
        out_specs=[
            pl.BlockSpec((groups_q, stride, head_size), lambda h: (0, 0, h)),
            pl.BlockSpec((groups_q, stride, BLOCK), lambda h: (0, 0, 0)),
        ],
        out_shape=[
            jax.ShapeDtypeStruct((groups_q, stride, width), jnp.float32),
            jax.ShapeDtypeStruct((groups_q, stride, BLOCK), jnp.float32),
        ],
        compiler_params=pltpu.CompilerParams(vmem_limit_bytes=48 * 1024 * 1024),
    )(all_q, qt, kv, kt, kv, vt, fl)


def body(q_img, k_img, v_img, q_txt, k_txt, v_txt, norm_gains, block_map):
    rows, width = q_img.shape
    head_size = norm_gains.shape[1]
    heads = width // head_size
    text_rows = q_txt.shape[0]
    stride = rows + text_rows
    groups_q = lax.axis_size("qq")
    groups_k = lax.axis_size("kk")
    own_q = lax.axis_index("qq")

    queries = jnp.concatenate(
        [normed(q_img, norm_gains[0], heads), normed(q_txt, norm_gains[2], heads)], axis=0
    ).reshape(1, stride, width)
    keys_image = normed(k_img, norm_gains[1], heads).reshape(1, rows, width)
    keys_text = normed(k_txt, norm_gains[3], heads).reshape(1, text_rows, width)
    pair = jnp.stack([keys_image, v_img.reshape(1, rows, width)], axis=0)
    text_pair = jnp.concatenate([keys_text, v_txt.reshape(1, text_rows, width)], axis=0)

    all_q = lax.all_gather(queries, "qq", axis=0, tiled=True)
    all_kv = lax.all_gather(pair, "kk", axis=1, tiled=True)
    text_spread = jnp.broadcast_to(text_pair[None], (groups_k,) + text_pair.shape)
    all_text = lax.all_to_all(text_spread, "kk", split_axis=0, concat_axis=0, tiled=True)
    flags = lax.all_gather(block_map, "qq", axis=1, tiled=True)
    flags = flags.reshape(heads, groups_q, groups_k, groups_q)
    flags = lax.dynamic_index_in_dim(flags, own_q, axis=3, keepdims=False)
    flags = jnp.repeat(flags, BLOCK, axis=2)

    qt = all_q[:, rows:].reshape(groups_q * text_rows, width)
    kt = all_text[:, 0].reshape(groups_k * text_rows, width)
    vt = all_text[:, 1].reshape(groups_k * text_rows, width)

    numer, denom = attend(all_q, qt, all_kv, kt, vt, flags, heads, head_size)
    denom = denom[:, :, :heads]
    denom_hi = denom.astype(jnp.bfloat16)
    denom_lo = (denom - denom_hi.astype(jnp.float32)).astype(jnp.bfloat16)
    sections = lax.axis_size("section")
    per = rows // sections
    count = sections * groups_q

    def by_destination(part):
        lanes = part.shape[2]
        image_rows = part[:, :rows].reshape(groups_q, per, sections, lanes).transpose(2, 0, 1, 3)
        text_part = jnp.broadcast_to(part[None, :, rows:], (sections, groups_q, text_rows, lanes))
        part = jnp.concatenate([image_rows, text_part], axis=2)
        return part.reshape(count, -1)

    flat_num = by_destination(numer.astype(jnp.bfloat16))
    flat_den = by_destination(jnp.concatenate([denom_hi, denom_lo], axis=2))
    num_size, den_size = flat_num.shape[1], flat_den.shape[1]
    total = num_size + den_size
    padded = -(-total // (16 * BLOCK)) * (16 * BLOCK)
    packed = jnp.concatenate(
        [flat_num, flat_den, jnp.zeros((count, padded - total), jnp.bfloat16)], axis=1
    ).reshape(count, padded // BLOCK, BLOCK)
    packed = lax.all_to_all(packed, ("section", "qq"), split_axis=0, concat_axis=0, tiled=True)
    packed = packed.reshape(sections, groups_q, padded)
    numer = jnp.sum(packed[:, :, :num_size].astype(jnp.float32), axis=1)
    numer = numer.reshape(sections, per + text_rows, heads, head_size)
    denom = jnp.sum(packed[:, :, num_size:total].astype(jnp.float32), axis=1)
    denom = denom.reshape(sections, per + text_rows, 2, heads)
    denom = denom[:, :, 0] + denom[:, :, 1]
    result = (numer / denom[..., None]).astype(jnp.bfloat16)
    image_out = result[:, :per].reshape(sections, per, width).transpose(1, 0, 2)
    image_out = image_out.reshape(per, 1, sections * width)
    own_section = lax.axis_index("section")
    text_out = lax.dynamic_index_in_dim(result[:, per:], own_section, axis=0, keepdims=False)
    text_out = text_out.reshape(text_rows, width)
    return (image_out, text_out)


def solution(mesh):
    sections, seq = mesh.devices.shape
    grid = Mesh(
        mesh.devices.reshape(sections, seq // QUERY_GROUP, QUERY_GROUP),
        ("section", "kk", "qq"),
    )
    rows = ("kk", "qq")
    placed = (
        P(rows, "section"),
        P(rows, "section"),
        P(rows, "section"),
        P(rows, "section"),
        P(rows, "section"),
        P(rows, "section"),
        P(),
        P("section", rows, None),
    )
    return jax.shard_map(
        body,
        mesh=grid,
        in_specs=placed,
        out_specs=(P(rows, "section", None), P(rows, "section")),
        check_vma=False,
    )
```

```python
import math

import jax
import jax.numpy as jnp
from jax import lax
from jax.experimental import pallas as pl
from jax.experimental.pallas import tpu as pltpu
from jax.sharding import Mesh, PartitionSpec as P

BLOCK = 128
QUERY_GROUP = 4


def normed(values, gain, heads):
    rows = values.shape[0]
    floats = values.astype(jnp.float32).reshape(rows, heads, gain.shape[0])
    power = jnp.mean(floats * floats, axis=-1, keepdims=True)
    return (floats * lax.rsqrt(power + 1e-06) * gain).astype(jnp.bfloat16)


def attend_kernel(q_ref, qt_ref, ki_ref, kt_ref, vi_ref, vt_ref, fl_ref, num_ref, den_ref):
    head = pl.program_id(0)
    head_size = q_ref.shape[-1]
    scale = head_size ** (-0.5) * math.log2(math.e)
    q_blocks = q_ref.shape[0]
    text_rows = qt_ref.shape[0] // q_blocks
    dims = (((1,), (1,)), ((), ()))
    keys_img = ki_ref[0].reshape(-1, head_size)
    keys_txt = kt_ref[...]
    vals_img = vi_ref[0].reshape(-1, head_size)
    vals_txt = vt_ref[...]

    @pl.when(head == 0)
    def _():
        den_ref[...] = jnp.zeros(den_ref.shape, den_ref.dtype)

    def one(q, flags):
        s_img = lax.dot_general(q, keys_img, dims, preferred_element_type=jnp.float32) * scale
        s_txt = lax.dot_general(q, keys_txt, dims, preferred_element_type=jnp.float32) * scale
        e_img = jnp.exp2(s_img)
        if flags is not None:
            e_img = jnp.where(flags > 0, e_img, jnp.float32(0.0))
        e_txt = jnp.exp2(s_txt)
        den = jnp.sum(e_img, axis=1, keepdims=True) + jnp.sum(e_txt, axis=1, keepdims=True)
        num = jnp.dot(e_img.astype(jnp.bfloat16), vals_img, preferred_element_type=jnp.float32)
        num = num + jnp.dot(e_txt.astype(jnp.bfloat16), vals_txt, preferred_element_type=jnp.float32)
        return num, den

    def put(a, lo, hi, num, den):
        num_ref[a, lo:hi, :] = num
        lane = lax.broadcasted_iota(jnp.int32, (hi - lo, den_ref.shape[-1]), 1)
        den_ref[a, lo:hi, :] = jnp.where(lane == head, den, den_ref[a, lo:hi, :])

    for a in range(q_blocks):
        num, den = one(q_ref[a, 0:BLOCK, :], fl_ref[0, a:a + 1, :])
        put(a, 0, BLOCK, num, den)
    num, den = one(qt_ref[...], None)
    for a in range(q_blocks):
        part = slice(a * text_rows, (a + 1) * text_rows)
        put(a, BLOCK, BLOCK + text_rows, num[part], den[part])


def attend(all_q, qt, kv, kt, vt, fl, heads, head_size):
    groups_q, stride = all_q.shape[0], all_q.shape[1]
    groups_k = kv.shape[1]
    n_qt, n_kt = qt.shape[0], kt.shape[0]
    width = heads * head_size

    def cols(rows):
        return pl.BlockSpec((rows, head_size), lambda h: (0, h))

    return pl.pallas_call(
        attend_kernel,
        grid=(heads,),
        in_specs=[
            pl.BlockSpec((groups_q, stride, head_size), lambda h: (0, 0, h)),
            cols(n_qt),
            pl.BlockSpec((1, groups_k, BLOCK, head_size), lambda h: (0, 0, 0, h)),
            cols(n_kt),
            pl.BlockSpec((1, groups_k, BLOCK, head_size), lambda h: (1, 0, 0, h)),
            cols(n_kt),
            pl.BlockSpec((1,) + fl.shape[1:], lambda h: (h, 0, 0)),
        ],
        out_specs=[
            pl.BlockSpec((groups_q, stride, head_size), lambda h: (0, 0, h)),
            pl.BlockSpec((groups_q, stride, BLOCK), lambda h: (0, 0, 0)),
        ],
        out_shape=[
            jax.ShapeDtypeStruct((groups_q, stride, width), jnp.float32),
            jax.ShapeDtypeStruct((groups_q, stride, BLOCK), jnp.float32),
        ],
        compiler_params=pltpu.CompilerParams(vmem_limit_bytes=48 * 1024 * 1024),
    )(all_q, qt, kv, kt, kv, vt, fl)


def body(q_img, k_img, v_img, q_txt, k_txt, v_txt, norm_gains, block_map):
    rows, width = q_img.shape
    head_size = norm_gains.shape[1]
    heads = width // head_size
    text_rows = q_txt.shape[0]
    stride = rows + text_rows
    groups_q = lax.axis_size("qq")
    groups_k = lax.axis_size("kk")
    own_q = lax.axis_index("qq")

    queries = jnp.concatenate(
        [normed(q_img, norm_gains[0], heads), normed(q_txt, norm_gains[2], heads)], axis=0
    ).reshape(1, stride, width)
    keys_image = normed(k_img, norm_gains[1], heads).reshape(1, rows, width)
    keys_text = normed(k_txt, norm_gains[3], heads).reshape(1, text_rows, width)
    pair = jnp.stack([keys_image, v_img.reshape(1, rows, width)], axis=0)
    text_pair = jnp.concatenate([keys_text, v_txt.reshape(1, text_rows, width)], axis=0)

    all_q = lax.all_gather(queries, "qq", axis=0, tiled=True)
    all_kv = lax.all_gather(pair, "kk", axis=1, tiled=True)
    text_spread = jnp.broadcast_to(text_pair[None], (groups_k,) + text_pair.shape)
    all_text = lax.all_to_all(text_spread, "kk", split_axis=0, concat_axis=0, tiled=True)
    flags = lax.all_gather(block_map, "qq", axis=1, tiled=True)
    flags = flags.reshape(heads, groups_q, groups_k, groups_q)
    flags = lax.dynamic_index_in_dim(flags, own_q, axis=3, keepdims=False)
    flags = jnp.repeat(flags, BLOCK, axis=2)

    qt = all_q[:, rows:].reshape(groups_q * text_rows, width)
    kt = all_text[:, 0].reshape(groups_k * text_rows, width)
    vt = all_text[:, 1].reshape(groups_k * text_rows, width)

    numer, denom = attend(all_q, qt, all_kv, kt, vt, flags, heads, head_size)
    denom = denom[:, :, :heads]
    denom_hi = denom.astype(jnp.bfloat16)
    denom_lo = (denom - denom_hi.astype(jnp.float32)).astype(jnp.bfloat16)
    sections = lax.axis_size("section")
    per = rows // sections
    count = sections * groups_q

    def by_destination(part):
        lanes = part.shape[2]
        image_rows = part[:, :rows].reshape(groups_q, per, sections, lanes).transpose(2, 0, 1, 3)
        text_part = jnp.broadcast_to(part[None, :, rows:], (sections, groups_q, text_rows, lanes))
        part = jnp.concatenate([image_rows, text_part], axis=2)
        return part.reshape(count, -1)

    flat_num = by_destination(numer.astype(jnp.bfloat16))
    flat_den = by_destination(jnp.concatenate([denom_hi, denom_lo], axis=2))
    num_size, den_size = flat_num.shape[1], flat_den.shape[1]
    total = num_size + den_size
    padded = -(-total // (16 * BLOCK)) * (16 * BLOCK)
    packed = jnp.concatenate(
        [flat_num, flat_den, jnp.zeros((count, padded - total), jnp.bfloat16)], axis=1
    ).reshape(count, padded // BLOCK, BLOCK)
    packed = lax.all_to_all(packed, ("section", "qq"), split_axis=0, concat_axis=0, tiled=True)
    packed = packed.reshape(sections, groups_q, padded)
    numer = jnp.sum(packed[:, :, :num_size].astype(jnp.float32), axis=1)
    numer = numer.reshape(sections, per + text_rows, heads, head_size)
    denom = jnp.sum(packed[:, :, num_size:total].astype(jnp.float32), axis=1)
    denom = denom.reshape(sections, per + text_rows, 2, heads)
    denom = denom[:, :, 0] + denom[:, :, 1]
    result = (numer / denom[..., None]).astype(jnp.bfloat16)
    image_out = result[:, :per].reshape(sections, per, width).transpose(1, 0, 2)
    image_out = image_out.reshape(per, 1, sections * width)
    own_section = lax.axis_index("section")
    text_out = lax.dynamic_index_in_dim(result[:, per:], own_section, axis=0, keepdims=False)
    text_out = text_out.reshape(text_rows, width)
    return (image_out, text_out)


def solution(mesh):
    sections, seq = mesh.devices.shape
    grid = Mesh(
        mesh.devices.reshape(sections, seq // QUERY_GROUP, QUERY_GROUP),
        ("section", "kk", "qq"),
    )
    rows = ("kk", "qq")
    placed = (
        P(rows, "section"),
        P(rows, "section"),
        P(rows, "section"),
        P(rows, "section"),
        P(rows, "section"),
        P(rows, "section"),
        P(),
        P("section", rows, None),
    )
    return jax.shard_map(
        body,
        mesh=grid,
        in_specs=placed,
        out_specs=(P(rows, "section", None), P(rows, "section")),
        check_vma=False,
    )
```
